32 devices in a mesh: strip: 8 (over z, core), slide: 4 (over y, x).
Axes of the slice: x: 2, y: 2, z: 4, core: 2. Of those that a mesh axis runs over, the one named last changes fastest.
Arguments:
- images: bfloat16 [4, 96, 48, 128], P('slide', None, 'strip'), may hold values from -6 to 6
- cotangent: bfloat16 [4, 96, 48, 128], P('slide', None, 'strip'), may hold values from -16 to 16
- conv_weight: float32 [96, 7, 7], replicated, may hold values from -0.875 to 0.875
- conv_bias: float32 [96], replicated, may hold values from -3 to 3
- norm_gain: float32 [96], replicated, may hold values from 0.5 to 1.5
- norm_bias: float32 [96], replicated, may hold values from -3 to 3
- up_weight: bfloat16 [96, 384], replicated, may hold values from -0.625 to 0.625
- up_bias: float32 [384], replicated, may hold values from -3 to 3
- down_weight: bfloat16 [384, 96], replicated, may hold values from -0.3125 to 0.3125
- down_bias: float32 [96], replicated, may hold values from -3 to 3
- layer_scale: float32 [96], replicated, may hold values from 0.5 to 1.5
Outputs:
- image_grad: bfloat16 [4, 96, 48, 128], P('slide', None, 'strip')
- conv_weight_grad: float32 [96, 7, 7], replicated
- conv_bias_grad: float32 [96], replicated
- norm_gain_grad: float32 [96], replicated
- norm_bias_grad: float32 [96], replicated
- up_weight_grad: float32 [96, 384], replicated
- up_bias_grad: float32 [384], replicated
- down_weight_grad: float32 [384, 96], replicated
- down_bias_grad: float32 [96], replicated
- layer_scale_grad: float32 [96], replicated
The draws below stay inside these ranges and needn't reach their ends.
All inputs are finite; a program needn't handle non-finite values.
Results may differ from the reference program's by a relative error of at most 0.0065.
Values may be sent and summed in bfloat16 or wider, within the bound.
No kernel may reach another device: no remote copies, remote signals or barrier semaphores. Data moves between devices by JAX's collectives and lax.ppermute only.
A program may use at most 64 MiB of HBM per device.

```python
import math
import jax
import jax.numpy as jnp
from jax import lax

C = 96
MLP_WIDTH = 384
KSIZE = 7
COLS = 128
ROWS = 48
SLIDES = 4


def draw_cotangent(key, part):
    base = jax.random.truncated_normal(key, -5.0, 5.0, (SLIDES, C, ROWS, COLS), jnp.float32)
    row_pos = jnp.arange(ROWS, dtype=jnp.float32) / ROWS
    slide_pos = jnp.arange(SLIDES, dtype=jnp.float32) / SLIDES
    ramp = jnp.exp(0.55 * (row_pos[None, None, :, None] + slide_pos[:, None, None, None]))
    return (base * ramp).astype(jnp.bfloat16)


def block_scale(own_key, extent, shards, least, largest):
    gain = 1.0
    for dim, shards_of in shards:
        heights = jax.random.uniform(jax.random.fold_in(jax.random.fold_in(own_key, 6), dim), (shards_of,), jnp.float32, least / len(shards), largest / len(shards))
        gain = gain * jnp.repeat(jnp.exp(heights), extent[dim] // shards_of).reshape((-1,) + (1,) * (len(extent) - 1 - dim))
    return gain


def scatter_about(rng, extent, scale, most, shards=(), held_as=jnp.bfloat16):
    array = jax.random.normal(rng, extent, jnp.float32) * scale
    if len(shards) > 0:
        array = block_scale(rng, extent, shards, -0.22, 0.18) * array
    return jnp.clip(array, min=-most, max=most).astype(held_as)


def setup_inputs(seed: int = 0) -> dict:
    seeds = jax.random.split(jax.random.key(seed), 12)
    images = scatter_about(seeds[0], (SLIDES, C, ROWS, COLS), 1.0, 6.0, ((0, 4), (2, 8)))
    cotangent = draw_cotangent(jax.random.fold_in(seeds[11], 71), 0)
    conv_weight = scatter_about(seeds[2], (C, KSIZE, KSIZE), (KSIZE * KSIZE) ** -0.5, 0.875, (), jnp.float32)
    conv_bias = scatter_about(seeds[3], (C,), 0.5, 3.0, (), jnp.float32)
    norm_gain = jnp.clip(jax.random.uniform(seeds[4], (C,), jnp.float32, 0.5, 1.5), 0.5, 1.5)
    norm_bias = scatter_about(seeds[5], (C,), 0.5, 3.0, (), jnp.float32)
    up_weight = scatter_about(seeds[6], (C, MLP_WIDTH), C ** -0.5, 0.625)
    up_bias = scatter_about(seeds[7], (MLP_WIDTH,), 0.5, 3.0, (), jnp.float32)
    down_weight = scatter_about(seeds[8], (MLP_WIDTH, C), MLP_WIDTH ** -0.5, 0.3125)
    down_bias = scatter_about(seeds[9], (C,), 0.5, 3.0, (), jnp.float32)
    layer_scale = jnp.clip(jax.random.uniform(seeds[10], (C,), jnp.float32, 0.5, 1.5), 0.5, 1.5)
    return {"images": images, "cotangent": cotangent, "conv_weight": conv_weight, "conv_bias": conv_bias, "norm_gain": norm_gain, "norm_bias": norm_bias, "up_weight": up_weight, "up_bias": up_bias, "down_weight": down_weight, "down_bias": down_bias, "layer_scale": layer_scale}


def rounded(value):
    return lax.optimization_barrier(value.astype(jnp.bfloat16)).astype(jnp.float32)

def gelu_slope(value):
    return 0.5 * (1.0 + jax.scipy.special.erf(value / math.sqrt(2.0))) + value * jnp.exp(-0.5 * value * value) / math.sqrt(2.0 * math.pi)

def reference(images, cotangent, conv_weight, conv_bias, norm_gain, norm_bias, up_weight, up_bias, down_weight, down_bias, layer_scale):
    up_full = up_weight.astype(jnp.float32)
    down_full = down_weight.astype(jnp.float32)

    def one_slide(pair):
        picture, upstream = pair
        padded = jnp.pad(picture.astype(jnp.float32), ((0, 0), (3, 3), (3, 3)))
        conv = jnp.zeros((C, ROWS, COLS), jnp.float32) + conv_bias[:, None, None]
        for a in range(KSIZE):
            for b in range(KSIZE):
                conv = conv + conv_weight[:, a, b][:, None, None] * padded[:, a:a + ROWS, b:b + COLS]
        centre = conv - lax.optimization_barrier(jnp.mean(conv, axis=0))
        inv = lax.rsqrt(lax.optimization_barrier(jnp.mean(centre * centre, axis=0)) + 1e-06)
        normed = centre * inv
        lifted = rounded(normed * norm_gain[:, None, None] + norm_bias[:, None, None])
        pre = jnp.einsum('crw,cf->frw', lifted, up_full) + up_bias[:, None, None]
        act = rounded(jax.nn.gelu(pre, approximate=False))
        branch = jnp.einsum('frw,fc->crw', act, down_full) + down_bias[:, None, None]
        upstream = upstream.astype(jnp.float32)
        d_branch = rounded(layer_scale[:, None, None] * upstream)
        d_act = jnp.einsum('crw,fc->frw', d_branch, down_full)
        d_pre = rounded(d_act * gelu_slope(pre))
        d_lifted = jnp.einsum('frw,cf->crw', d_pre, up_full)
        d_normed = d_lifted * norm_gain[:, None, None]
        d_conv = inv * (d_normed - lax.optimization_barrier(jnp.mean(d_normed, axis=0)) - normed * lax.optimization_barrier(jnp.mean(d_normed * normed, axis=0)))
        d_padded = jnp.pad(d_conv, ((0, 0), (3, 3), (3, 3)))
        image_grad = upstream
        taps = []
        for a in range(KSIZE):
            for b in range(KSIZE):
                image_grad = image_grad + conv_weight[:, a, b][:, None, None] * d_padded[:, 6 - a:6 - a + ROWS, 6 - b:6 - b + COLS]
                taps.append(lax.optimization_barrier(jnp.sum(d_conv * padded[:, a:a + ROWS, b:b + COLS], axis=(1, 2))))
        kernel_grad = jnp.stack(taps, axis=1).reshape(C, KSIZE, KSIZE)
        sums = (kernel_grad, lax.optimization_barrier(jnp.sum(d_conv, axis=(1, 2))), lax.optimization_barrier(jnp.sum(d_lifted * normed, axis=(1, 2))), lax.optimization_barrier(jnp.sum(d_lifted, axis=(1, 2))), jnp.einsum('crw,frw->cf', lifted, d_pre), lax.optimization_barrier(jnp.sum(d_pre, axis=(1, 2))), jnp.einsum('frw,crw->fc', act, d_branch), lax.optimization_barrier(jnp.sum(d_branch, axis=(1, 2))), lax.optimization_barrier(jnp.sum(upstream * branch, axis=(1, 2))))
        return (image_grad.astype(jnp.bfloat16), sums)
    image_grad, sums = lax.map(one_slide, (images, cotangent))
    scale = 1.0 / math.sqrt(float(SLIDES * ROWS * COLS))
    g = [lax.optimization_barrier(jnp.sum(item, axis=0)) * scale for item in sums]
    return (image_grad, g[0], g[1], g[2], g[3], g[4], g[5], g[6], g[7], g[8])
```

```python
import math

import jax
import jax.numpy as jnp
from jax import lax
from jax.sharding import PartitionSpec as P


def with_halo(array, sides, width):
    for axis, dim in sides:
        size, length = (lax.axis_size(axis), array.shape[dim])
        up = [(i, (i + 1) % size) for i in range(size - 1)]
        down = [(j, i) for i, j in up]
        last = lax.slice_in_dim(array, length - width, length, axis=dim)
        first = lax.slice_in_dim(array, 0, width, axis=dim)
        before = lax.ppermute(last, axis, up)
        after = lax.ppermute(first, axis, down)
        array = jnp.concatenate([before, array, after], axis=dim)
    return array


def butterfly_steps(axes):
    steps = []
    for axis in axes:
        size = lax.axis_size(axis)
        bit = 1
        while bit < size:
            steps.append((axis, bit))
            bit *= 2
    order = {"strip": 0, "slide": 1}
    steps.sort(key=lambda s: (0 if (s[0] == "strip" and s[1] == 1) else 1, s[1], order[s[0]]))
    return steps


def tree_psum(terms, axes):
    shapes = [t.shape for t in terms]
    sizes = [math.prod(s) for s in shapes]
    total = sum(sizes)
    steps = butterfly_steps(axes)
    pieces = 2 ** len(steps)
    rows = -(-total // (pieces * 128))
    rows = -(-rows // 8) * 8
    flat = jnp.concatenate([t.reshape(-1) for t in terms])
    flat = jnp.pad(flat, (0, pieces * rows * 128 - total)).reshape(pieces, rows, 128)
    for axis, bit in steps:
        size = lax.axis_size(axis)
        half = flat.shape[0] // 2
        mine = (lax.axis_index(axis) // bit) % 2
        keep = lax.dynamic_slice_in_dim(flat, mine * half, half, axis=0)
        give = lax.dynamic_slice_in_dim(flat, (1 - mine) * half, half, axis=0)
        got = lax.ppermute(give, axis, [(i, i ^ bit) for i in range(size)])
        flat = keep + got
    for axis, bit in reversed(steps):
        size = lax.axis_size(axis)
        mine = (lax.axis_index(axis) // bit) % 2
        got = lax.ppermute(flat, axis, [(i, i ^ bit) for i in range(size)])
        low = jnp.where(mine == 0, flat, got)
        high = jnp.where(mine == 0, got, flat)
        flat = jnp.concatenate([low, high], axis=0)
    flat = flat.reshape(-1)
    out = []
    offset = 0
    for shape, size in zip(shapes, sizes):
        out.append(flat[offset : offset + size].reshape(shape))
        offset += size
    return out

def gelu_slope(value):
    return 0.5 * (1.0 + jax.scipy.special.erf(value / math.sqrt(2.0))) + value * jnp.exp(
        -0.5 * value * value
    ) / math.sqrt(2.0 * math.pi)


def on_device(
    images,
    cotangent,
    conv_weight,
    conv_bias,
    norm_gain,
    norm_bias,
    up_weight,
    up_bias,
    down_weight,
    down_bias,
    layer_scale,
):
    slides_here = images.shape[0]
    chans = images.shape[1]
    rows = images.shape[2]
    cols = images.shape[3]
    kernel = conv_weight.shape[1]
    extended = with_halo(images, (("strip", 2),), 3)
    upstream = cotangent.astype(jnp.float32)
    padded = jnp.pad(extended, ((0, 0), (0, 0), (0, 0), (3, 3)))
    conv = jnp.zeros((slides_here, chans, rows, cols), jnp.float32) + conv_bias[None, :, None, None]
    for a in range(kernel):
        for b in range(kernel):
            conv = (
                conv
                + conv_weight[:, a, b][None, :, None, None]
                * padded[:, :, a : a + rows, b : b + cols]
            )
    centre = conv - jnp.mean(conv, axis=1, keepdims=True)
    inv = lax.rsqrt(jnp.mean(centre * centre, axis=1, keepdims=True) + 1e-06)
    normed = centre * inv
    lifted = (normed * norm_gain[None, :, None, None] + norm_bias[None, :, None, None]).astype(
        jnp.bfloat16
    )
    pre = (
        jnp.einsum("scrw,cf->sfrw", lifted, up_weight, preferred_element_type=jnp.float32)
        + up_bias[None, :, None, None]
    )
    act = jax.nn.gelu(pre, approximate=False).astype(jnp.bfloat16)
    branch = (
        jnp.einsum("sfrw,fc->scrw", act, down_weight, preferred_element_type=jnp.float32)
        + down_bias[None, :, None, None]
    )
    d_branch = (layer_scale[None, :, None, None] * upstream).astype(jnp.bfloat16)
    d_act = jnp.einsum("scrw,fc->sfrw", d_branch, down_weight, preferred_element_type=jnp.float32)
    d_pre = (d_act * gelu_slope(pre)).astype(jnp.bfloat16)
    d_lifted = jnp.einsum("sfrw,cf->scrw", d_pre, up_weight, preferred_element_type=jnp.float32)
    d_normed = d_lifted * norm_gain[None, :, None, None]
    d_conv = inv * (
        d_normed
        - jnp.mean(d_normed, axis=1, keepdims=True)
        - normed * jnp.mean(d_normed * normed, axis=1, keepdims=True)
    )
    d_wide = with_halo(d_conv, (("strip", 2),), 3)
    d_padded = jnp.pad(d_wide, ((0, 0), (0, 0), (0, 0), (3, 3)))
    image_grad = cotangent.astype(jnp.float32)
    taps = []
    for a in range(kernel):
        for b in range(kernel):
            image_grad = (
                image_grad
                + conv_weight[:, a, b][None, :, None, None]
                * d_padded[:, :, 6 - a : 6 - a + rows, 6 - b : 6 - b + cols]
            )
            taps.append(jnp.sum(d_conv * padded[:, :, a : a + rows, b : b + cols], axis=(0, 2, 3)))
    kernel_grad = jnp.stack(taps, axis=1).reshape(chans, kernel, kernel)
    terms = (
        kernel_grad,
        jnp.sum(d_conv, axis=(0, 2, 3)),
        jnp.sum(d_lifted * normed, axis=(0, 2, 3)),
        jnp.sum(d_lifted, axis=(0, 2, 3)),
        jnp.einsum("scrw,sfrw->cf", lifted, d_pre, preferred_element_type=jnp.float32),
        jnp.sum(d_pre.astype(jnp.float32), axis=(0, 2, 3)),
        jnp.einsum("sfrw,scrw->fc", act, d_branch, preferred_element_type=jnp.float32),
        jnp.sum(d_branch.astype(jnp.float32), axis=(0, 2, 3)),
        jnp.sum(upstream * branch, axis=(0, 2, 3)),
    )
    pixel_count = slides_here * lax.axis_size("slide") * rows * lax.axis_size("strip") * cols
    scale = 1.0 / math.sqrt(float(pixel_count))
    g = tree_psum(terms, ("strip", "slide"))
    g = [item * scale for item in g]
    return (image_grad.astype(jnp.bfloat16), g[0], g[1], g[2], g[3], g[4], g[5], g[6], g[7], g[8])


def solution(mesh):
    in_specs = (
        P("slide", None, "strip", None),
        P("slide", None, "strip", None),
        P(),
        P(),
        P(),
        P(),
        P(),
        P(),
        P(),
        P(),
        P(),
    )
    out_specs = (P("slide", None, "strip", None), P(), P(), P(), P(), P(), P(), P(), P(), P())
    return jax.shard_map(
        on_device, mesh=mesh, in_specs=in_specs, out_specs=out_specs, check_vma=False
    )
```

```python
import math

import jax
import jax.numpy as jnp
from jax import lax
from jax.sharding import PartitionSpec as P


def with_halo(array, sides, width):
    for axis, dim in sides:
        size, length = (lax.axis_size(axis), array.shape[dim])
        up = [(i, (i + 1) % size) for i in range(size - 1)]
        down = [(j, i) for i, j in up]
        last = lax.slice_in_dim(array, length - width, length, axis=dim)
        first = lax.slice_in_dim(array, 0, width, axis=dim)
        before = lax.ppermute(last, axis, up)
        after = lax.ppermute(first, axis, down)
        array = jnp.concatenate([before, array, after], axis=dim)
    return array


def xor_pairs(size, mask):
    return [(i, i ^ mask) for i in range(size)]


def low_bits(size):
    bits = []
    bit = 1
    while bit < size:
        bits.append(bit)
        bit *= 2
    return bits


def tree_psum(terms):
    shapes = [t.shape for t in terms]
    sizes = [math.prod(s) for s in shapes]
    total = sum(sizes)
    strip_bits = low_bits(lax.axis_size("strip"))
    slide_bits = low_bits(lax.axis_size("slide"))
    scatter = [("strip", b) for b in strip_bits[:2]]
    stages = [("slide", slide_bits[i : i + 2]) for i in range(0, len(slide_bits), 2)]
    stages += [("strip", [b]) for b in strip_bits[2:]]
    pieces = 2 ** len(scatter)
    rows = -(-total // (pieces * 128))
    rows = -(-rows // 8) * 8
    flat = jnp.concatenate([t.reshape(-1) for t in terms])
    flat = jnp.pad(flat, (0, pieces * rows * 128 - total)).reshape(pieces, rows, 128)
    for axis, bit in scatter:
        size = lax.axis_size(axis)
        half = flat.shape[0] // 2
        mine = (lax.axis_index(axis) // bit) % 2
        keep = lax.dynamic_slice_in_dim(flat, mine * half, half, axis=0)
        give = lax.dynamic_slice_in_dim(flat, (1 - mine) * half, half, axis=0)
        flat = keep + lax.ppermute(give, axis, xor_pairs(size, bit))
    for axis, bits in stages:
        size = lax.axis_size(axis)
        masks = []
        for m in range(1, 2 ** len(bits)):
            masks.append(sum(b for k, b in enumerate(bits) if (m >> k) & 1))
        got = [lax.ppermute(flat, axis, xor_pairs(size, mask)) for mask in masks]
        for item in got:
            flat = flat + item
    for axis, bit in reversed(scatter):
        size = lax.axis_size(axis)
        mine = (lax.axis_index(axis) // bit) % 2
        got = lax.ppermute(flat, axis, xor_pairs(size, bit))
        low = jnp.where(mine == 0, flat, got)
        high = jnp.where(mine == 0, got, flat)
        flat = jnp.concatenate([low, high], axis=0)
    flat = flat.reshape(-1)
    out = []
    offset = 0
    for shape, size in zip(shapes, sizes):
        out.append(flat[offset : offset + size].reshape(shape))
        offset += size
    return out


def gelu_slope(value):
    return 0.5 * (1.0 + jax.scipy.special.erf(value / math.sqrt(2.0))) + value * jnp.exp(
        -0.5 * value * value
    ) / math.sqrt(2.0 * math.pi)


def on_device(
    images,
    cotangent,
    conv_weight,
    conv_bias,
    norm_gain,
    norm_bias,
    up_weight,
    up_bias,
    down_weight,
    down_bias,
    layer_scale,
):
    slides_here = images.shape[0]
    chans = images.shape[1]
    rows = images.shape[2]
    cols = images.shape[3]
    kernel = conv_weight.shape[1]
    extended = with_halo(images, (("strip", 2),), 3)
    upstream = cotangent.astype(jnp.float32)
    padded = jnp.pad(extended, ((0, 0), (0, 0), (0, 0), (3, 3)))
    conv = jnp.zeros((slides_here, chans, rows, cols), jnp.float32) + conv_bias[None, :, None, None]
    for a in range(kernel):
        for b in range(kernel):
            conv = (
                conv
                + conv_weight[:, a, b][None, :, None, None]
                * padded[:, :, a : a + rows, b : b + cols]
            )
    centre = conv - jnp.mean(conv, axis=1, keepdims=True)
    inv = lax.rsqrt(jnp.mean(centre * centre, axis=1, keepdims=True) + 1e-06)
    normed = centre * inv
    lifted = (normed * norm_gain[None, :, None, None] + norm_bias[None, :, None, None]).astype(
        jnp.bfloat16
    )
    pre = (
        jnp.einsum("scrw,cf->sfrw", lifted, up_weight, preferred_element_type=jnp.float32)
        + up_bias[None, :, None, None]
    )
    act = jax.nn.gelu(pre, approximate=False).astype(jnp.bfloat16)
    branch = (
        jnp.einsum("sfrw,fc->scrw", act, down_weight, preferred_element_type=jnp.float32)
        + down_bias[None, :, None, None]
    )
    d_branch = (layer_scale[None, :, None, None] * upstream).astype(jnp.bfloat16)
    d_act = jnp.einsum("scrw,fc->sfrw", d_branch, down_weight, preferred_element_type=jnp.float32)
    d_pre = (d_act * gelu_slope(pre)).astype(jnp.bfloat16)
    d_lifted = jnp.einsum("sfrw,cf->scrw", d_pre, up_weight, preferred_element_type=jnp.float32)
    d_normed = d_lifted * norm_gain[None, :, None, None]
    d_conv = inv * (
        d_normed
        - jnp.mean(d_normed, axis=1, keepdims=True)
        - normed * jnp.mean(d_normed * normed, axis=1, keepdims=True)
    )
    d_wide = with_halo(d_conv, (("strip", 2),), 3)
    d_padded = jnp.pad(d_wide, ((0, 0), (0, 0), (0, 0), (3, 3)))
    image_grad = cotangent.astype(jnp.float32)
    taps = []
    for a in range(kernel):
        for b in range(kernel):
            image_grad = (
                image_grad
                + conv_weight[:, a, b][None, :, None, None]
                * d_padded[:, :, 6 - a : 6 - a + rows, 6 - b : 6 - b + cols]
            )
            taps.append(jnp.sum(d_conv * padded[:, :, a : a + rows, b : b + cols], axis=(0, 2, 3)))
    kernel_grad = jnp.stack(taps, axis=1).reshape(chans, kernel, kernel)
    terms = (
        kernel_grad,
        jnp.sum(d_conv, axis=(0, 2, 3)),
        jnp.sum(d_lifted * normed, axis=(0, 2, 3)),
        jnp.sum(d_lifted, axis=(0, 2, 3)),
        jnp.einsum("scrw,sfrw->cf", lifted, d_pre, preferred_element_type=jnp.float32),
        jnp.sum(d_pre.astype(jnp.float32), axis=(0, 2, 3)),
        jnp.einsum("sfrw,scrw->fc", act, d_branch, preferred_element_type=jnp.float32),
        jnp.sum(d_branch.astype(jnp.float32), axis=(0, 2, 3)),
        jnp.sum(upstream * branch, axis=(0, 2, 3)),
    )
    pixel_count = slides_here * lax.axis_size("slide") * rows * lax.axis_size("strip") * cols
    scale = 1.0 / math.sqrt(float(pixel_count))
    g = tree_psum(terms)
    g = [item * scale for item in g]
    return (image_grad.astype(jnp.bfloat16), g[0], g[1], g[2], g[3], g[4], g[5], g[6], g[7], g[8])


def solution(mesh):
    in_specs = (
        P("slide", None, "strip", None),
        P("slide", None, "strip", None),
        P(),
        P(),
        P(),
        P(),
        P(),
        P(),
        P(),
        P(),
        P(),
    )
    out_specs = (P("slide", None, "strip", None), P(), P(), P(), P(), P(), P(), P(), P(), P())
    return jax.shard_map(
        on_device, mesh=mesh, in_specs=in_specs, out_specs=out_specs, check_vma=False
    )
```

```python
import math

import jax
import jax.numpy as jnp
from jax import lax
from jax.sharding import PartitionSpec as P


def with_halo(array, sides, width):
    for axis, dim in sides:
        size, length = (lax.axis_size(axis), array.shape[dim])
        up = [(i, (i + 1) % size) for i in range(size - 1)]
        down = [(j, i) for i, j in up]
        last = lax.slice_in_dim(array, length - width, length, axis=dim)
        first = lax.slice_in_dim(array, 0, width, axis=dim)
        before = lax.ppermute(last, axis, up)
        after = lax.ppermute(first, axis, down)
        array = jnp.concatenate([before, array, after], axis=dim)
    return array


def xor_pairs(size, mask):
    return [(i, i ^ mask) for i in range(size)]


def low_bits(size):
    bits = []
    bit = 1
    while bit < size:
        bits.append(bit)
        bit *= 2
    return bits


def tree_psum(terms):
    shapes = [t.shape for t in terms]
    sizes = [math.prod(s) for s in shapes]
    rooms = [-(-size // 1024) * 1024 for size in sizes]
    total = sum(rooms)
    strip_bits = low_bits(lax.axis_size("strip"))
    slide_bits = low_bits(lax.axis_size("slide"))
    scatter = [("strip", b) for b in strip_bits[:2]]
    stages = [("slide", slide_bits[i : i + 2]) for i in range(0, len(slide_bits), 2)]
    stages += [("strip", [b]) for b in strip_bits[2:]]
    pieces = 2 ** len(scatter)
    rows = -(-total // (pieces * 128))
    rows = -(-rows // 8) * 8
    flat = jnp.concatenate([jnp.pad(t.reshape(-1), (0, room - size)) for t, size, room in zip(terms, sizes, rooms)])
    flat = jnp.pad(flat, (0, pieces * rows * 128 - total)).reshape(pieces, rows, 128)
    for axis, bit in scatter:
        size = lax.axis_size(axis)
        half = flat.shape[0] // 2
        mine = (lax.axis_index(axis) // bit) % 2
        keep = lax.dynamic_slice_in_dim(flat, mine * half, half, axis=0)
        give = lax.dynamic_slice_in_dim(flat, (1 - mine) * half, half, axis=0)
        flat = keep + lax.ppermute(give, axis, xor_pairs(size, bit))
    for axis, bits in stages:
        size = lax.axis_size(axis)
        masks = []
        for m in range(1, 2 ** len(bits)):
            masks.append(sum(b for k, b in enumerate(bits) if (m >> k) & 1))
        got = [lax.ppermute(flat, axis, xor_pairs(size, mask)) for mask in masks]
        for item in got:
            flat = flat + item
    for axis, bit in reversed(scatter):
        size = lax.axis_size(axis)
        mine = (lax.axis_index(axis) // bit) % 2
        got = lax.ppermute(flat, axis, xor_pairs(size, bit))
        low = jnp.where(mine == 0, flat, got)
        high = jnp.where(mine == 0, got, flat)
        flat = jnp.concatenate([low, high], axis=0)
    flat = flat.reshape(-1)
    out = []
    offset = 0
    for shape, size, room in zip(shapes, sizes, rooms):
        out.append(flat[offset : offset + size].reshape(shape))
        offset += room
    return out


def gelu_slope(value):
    return 0.5 * (1.0 + jax.scipy.special.erf(value / math.sqrt(2.0))) + value * jnp.exp(
        -0.5 * value * value
    ) / math.sqrt(2.0 * math.pi)


def on_device(
    images,
    cotangent,
    conv_weight,
    conv_bias,
    norm_gain,
    norm_bias,
    up_weight,
    up_bias,
    down_weight,
    down_bias,
    layer_scale,
):
    slides_here = images.shape[0]
    chans = images.shape[1]
    rows = images.shape[2]
    cols = images.shape[3]
    kernel = conv_weight.shape[1]
    extended = with_halo(images, (("strip", 2),), 3)
    upstream = cotangent.astype(jnp.float32)
    padded = jnp.pad(extended, ((0, 0), (0, 0), (0, 0), (3, 3)))
    conv = jnp.zeros((slides_here, chans, rows, cols), jnp.float32) + conv_bias[None, :, None, None]
    for a in range(kernel):
        for b in range(kernel):
            conv = (
                conv
                + conv_weight[:, a, b][None, :, None, None]
                * padded[:, :, a : a + rows, b : b + cols]
            )
    centre = conv - jnp.mean(conv, axis=1, keepdims=True)
    inv = lax.rsqrt(jnp.mean(centre * centre, axis=1, keepdims=True) + 1e-06)
    normed = centre * inv
    lifted = (normed * norm_gain[None, :, None, None] + norm_bias[None, :, None, None]).astype(
        jnp.bfloat16
    )
    pre = (
        jnp.einsum("scrw,cf->sfrw", lifted, up_weight, preferred_element_type=jnp.float32)
        + up_bias[None, :, None, None]
    )
    act = jax.nn.gelu(pre, approximate=False).astype(jnp.bfloat16)
    branch = (
        jnp.einsum("sfrw,fc->scrw", act, down_weight, preferred_element_type=jnp.float32)
        + down_bias[None, :, None, None]
    )
    d_branch = (layer_scale[None, :, None, None] * upstream).astype(jnp.bfloat16)
    d_act = jnp.einsum("scrw,fc->sfrw", d_branch, down_weight, preferred_element_type=jnp.float32)
    d_pre = (d_act * gelu_slope(pre)).astype(jnp.bfloat16)
    d_lifted = jnp.einsum("sfrw,cf->scrw", d_pre, up_weight, preferred_element_type=jnp.float32)
    d_normed = d_lifted * norm_gain[None, :, None, None]
    d_conv = inv * (
        d_normed
        - jnp.mean(d_normed, axis=1, keepdims=True)
        - normed * jnp.mean(d_normed * normed, axis=1, keepdims=True)
    )
    d_wide = with_halo(d_conv, (("strip", 2),), 3)
    d_padded = jnp.pad(d_wide, ((0, 0), (0, 0), (0, 0), (3, 3)))
    image_grad = cotangent.astype(jnp.float32)
    taps = []
    for a in range(kernel):
        for b in range(kernel):
            image_grad = (
                image_grad
                + conv_weight[:, a, b][None, :, None, None]
                * d_padded[:, :, 6 - a : 6 - a + rows, 6 - b : 6 - b + cols]
            )
            taps.append(jnp.sum(d_conv * padded[:, :, a : a + rows, b : b + cols], axis=(0, 2, 3)))
    pixel_count = slides_here * lax.axis_size("slide") * rows * lax.axis_size("strip") * cols
    scale = 1.0 / math.sqrt(float(pixel_count))
    terms = (
        jnp.stack(taps, axis=0),
        jnp.sum(d_conv, axis=(0, 2, 3)),
        jnp.sum(d_lifted * normed, axis=(0, 2, 3)),
        jnp.sum(d_lifted, axis=(0, 2, 3)),
        jnp.einsum("scrw,sfrw->cf", lifted, d_pre, preferred_element_type=jnp.float32),
        jnp.sum(d_pre.astype(jnp.float32), axis=(0, 2, 3)),
        jnp.einsum("scrw,sfrw->cf", d_branch, act, preferred_element_type=jnp.float32),
        jnp.sum(d_branch.astype(jnp.float32), axis=(0, 2, 3)),
        jnp.sum(upstream * branch, axis=(0, 2, 3)),
    )
    g = tree_psum([item * scale for item in terms])
    g[0] = g[0].reshape(kernel, kernel, chans).transpose(2, 0, 1)
    g[6] = g[6].T
    return (image_grad.astype(jnp.bfloat16), g[0], g[1], g[2], g[3], g[4], g[5], g[6], g[7], g[8])


def solution(mesh):
    in_specs = (
        P("slide", None, "strip", None),
        P("slide", None, "strip", None),
        P(),
        P(),
        P(),
        P(),
        P(),
        P(),
        P(),
        P(),
        P(),
    )
    out_specs = (P("slide", None, "strip", None), P(), P(), P(), P(), P(), P(), P(), P(), P())
    return jax.shard_map(
        on_device, mesh=mesh, in_specs=in_specs, out_specs=out_specs, check_vma=False
    )
```

```python
import math

import jax
import jax.numpy as jnp
from jax import lax
from jax.sharding import PartitionSpec as P


def with_halo(array, sides, width):
    for axis, dim in sides:
        size, length = (lax.axis_size(axis), array.shape[dim])
        up = [(i, (i + 1) % size) for i in range(size - 1)]
        down = [(j, i) for i, j in up]
        last = lax.slice_in_dim(array, length - width, length, axis=dim)
        first = lax.slice_in_dim(array, 0, width, axis=dim)
        before = lax.ppermute(last, axis, up)
        after = lax.ppermute(first, axis, down)
        array = jnp.concatenate([before, array, after], axis=dim)
    return array


def xor_pairs(size, mask):
    return [(i, i ^ mask) for i in range(size)]


def low_bits(size):
    bits = []
    bit = 1
    while bit < size:
        bits.append(bit)
        bit *= 2
    return bits


def tree_psum(terms):
    shapes = [t.shape for t in terms]
    sizes = [math.prod(s) for s in shapes]
    rooms = [-(-size // 1024) * 1024 for size in sizes]
    total = sum(rooms)
    strip_bits = low_bits(lax.axis_size("strip"))
    slide_bits = low_bits(lax.axis_size("slide"))
    scatter = [("strip", b) for b in strip_bits[:2]]
    stages = [("slide", slide_bits[i : i + 2]) for i in range(0, len(slide_bits), 2)]
    stages += [("strip", [b]) for b in strip_bits[2:]]
    pieces = 2 ** len(scatter)
    rows = -(-total // (pieces * 128))
    rows = -(-rows // 8) * 8
    flat = jnp.concatenate([jnp.pad(t.reshape(-1), (0, room - size)) for t, size, room in zip(terms, sizes, rooms)])
    flat = jnp.pad(flat, (0, pieces * rows * 128 - total)).reshape(pieces, rows, 128)
    for axis, bit in scatter:
        size = lax.axis_size(axis)
        half = flat.shape[0] // 2
        mine = (lax.axis_index(axis) // bit) % 2
        keep = lax.dynamic_slice_in_dim(flat, mine * half, half, axis=0)
        give = lax.dynamic_slice_in_dim(flat, (1 - mine) * half, half, axis=0)
        flat = keep + lax.ppermute(give, axis, xor_pairs(size, bit))
    for axis, bits in stages:
        size = lax.axis_size(axis)
        masks = []
        for m in range(1, 2 ** len(bits)):
            masks.append(sum(b for k, b in enumerate(bits) if (m >> k) & 1))
        got = [lax.ppermute(flat, axis, xor_pairs(size, mask)) for mask in masks]
        for item in got:
            flat = flat + item
    for axis, bit in reversed(scatter):
        size = lax.axis_size(axis)
        mine = (lax.axis_index(axis) // bit) % 2
        got = lax.ppermute(flat, axis, xor_pairs(size, bit))
        low = jnp.where(mine == 0, flat, got)
        high = jnp.where(mine == 0, got, flat)
        flat = jnp.concatenate([low, high], axis=0)
    flat = flat.reshape(-1)
    out = []
    offset = 0
    for shape, size, room in zip(shapes, sizes, rooms):
        out.append(flat[offset : offset + size].reshape(shape))
        offset += room
    return out


def gelu_slope(value):
    return 0.5 * (1.0 + jax.scipy.special.erf(value / math.sqrt(2.0))) + value * jnp.exp(
        -0.5 * value * value
    ) / math.sqrt(2.0 * math.pi)


def on_device(
    images,
    cotangent,
    conv_weight,
    conv_bias,
    norm_gain,
    norm_bias,
    up_weight,
    up_bias,
    down_weight,
    down_bias,
    layer_scale,
):
    slides_here = images.shape[0]
    chans = images.shape[1]
    rows = images.shape[2]
    cols = images.shape[3]
    kernel = conv_weight.shape[1]
    extended = with_halo(images, (("strip", 2),), 3)
    upstream = cotangent.astype(jnp.float32)
    padded = jnp.pad(extended, ((0, 0), (0, 0), (0, 0), (3, 3)))
    conv = jnp.zeros((slides_here, chans, rows, cols), jnp.float32) + conv_bias[None, :, None, None]
    for a in range(kernel):
        for b in range(kernel):
            conv = (
                conv
                + conv_weight[:, a, b][None, :, None, None]
                * padded[:, :, a : a + rows, b : b + cols]
            )
    centre = conv - jnp.mean(conv, axis=1, keepdims=True)
    inv = lax.rsqrt(jnp.mean(centre * centre, axis=1, keepdims=True) + 1e-06)
    normed = centre * inv
    lifted = (normed * norm_gain[None, :, None, None] + norm_bias[None, :, None, None]).astype(
        jnp.bfloat16
    )
    pre = (
        jnp.einsum("scrw,cf->sfrw", lifted, up_weight, preferred_element_type=jnp.float32)
        + up_bias[None, :, None, None]
    )
    act = jax.nn.gelu(pre, approximate=False).astype(jnp.bfloat16)
    branch = (
        jnp.einsum("sfrw,fc->scrw", act, down_weight, preferred_element_type=jnp.float32)
        + down_bias[None, :, None, None]
    )
    d_branch = (layer_scale[None, :, None, None] * upstream).astype(jnp.bfloat16)
    d_act = jnp.einsum("scrw,fc->sfrw", d_branch, down_weight, preferred_element_type=jnp.float32)
    d_pre = (d_act * gelu_slope(pre)).astype(jnp.bfloat16)
    d_lifted = jnp.einsum("sfrw,cf->scrw", d_pre, up_weight, preferred_element_type=jnp.float32)
    d_normed = d_lifted * norm_gain[None, :, None, None]
    d_conv = inv * (
        d_normed
        - jnp.mean(d_normed, axis=1, keepdims=True)
        - normed * jnp.mean(d_normed * normed, axis=1, keepdims=True)
    )
    d_wide = with_halo(d_conv, (("strip", 2),), 3)
    d_padded = jnp.pad(d_wide, ((0, 0), (0, 0), (0, 0), (3, 3)))
    image_grad = cotangent.astype(jnp.float32)
    taps = []
    for a in range(kernel):
        for b in range(kernel):
            image_grad = (
                image_grad
                + conv_weight[:, a, b][None, :, None, None]
                * d_padded[:, :, 6 - a : 6 - a + rows, 6 - b : 6 - b + cols]
            )
            taps.append(jnp.sum(d_conv * padded[:, :, a : a + rows, b : b + cols], axis=(0, 2, 3)))
    pixel_count = slides_here * lax.axis_size("slide") * rows * lax.axis_size("strip") * cols
    scale = 1.0 / math.sqrt(float(pixel_count))
    terms = (
        jnp.stack(taps, axis=0),
        jnp.sum(d_conv, axis=(0, 2, 3)),
        jnp.sum(d_lifted * normed, axis=(0, 2, 3)),
        jnp.sum(d_lifted, axis=(0, 2, 3)),
        jnp.einsum("scrw,sfrw->cf", lifted, d_pre, preferred_element_type=jnp.float32),
        jnp.sum(d_pre.astype(jnp.float32), axis=(0, 2, 3)),
        jnp.einsum("scrw,sfrw->cf", d_branch, act, preferred_element_type=jnp.float32),
        jnp.sum(d_branch.astype(jnp.float32), axis=(0, 2, 3)),
        jnp.sum(upstream * branch, axis=(0, 2, 3)),
    )
    early = tree_psum([terms[i] * scale for i in (6, 7, 8)])
    late = tree_psum([terms[i] * scale for i in (0, 1, 2, 3, 4, 5)])
    g = late + early
    g[0] = g[0].reshape(kernel, kernel, chans).transpose(2, 0, 1)
    g[6] = g[6].T
    return (image_grad.astype(jnp.bfloat16), g[0], g[1], g[2], g[3], g[4], g[5], g[6], g[7], g[8])


def solution(mesh):
    in_specs = (
        P("slide", None, "strip", None),
        P("slide", None, "strip", None),
        P(),
        P(),
        P(),
        P(),
        P(),
        P(),
        P(),
        P(),
        P(),
    )
    out_specs = (P("slide", None, "strip", None), P(), P(), P(), P(), P(), P(), P(), P(), P())
    return jax.shard_map(
        on_device, mesh=mesh, in_specs=in_specs, out_specs=out_specs, check_vma=False
    )
```

```python
import math

import jax
import jax.numpy as jnp
from jax import lax
from jax.sharding import PartitionSpec as P


def with_halo(array, sides, width):
    for axis, dim in sides:
        size, length = (lax.axis_size(axis), array.shape[dim])
        up = [(i, (i + 1) % size) for i in range(size - 1)]
        down = [(j, i) for i, j in up]
        last = lax.slice_in_dim(array, length - width, length, axis=dim)
        first = lax.slice_in_dim(array, 0, width, axis=dim)
        before = lax.ppermute(last, axis, up)
        after = lax.ppermute(first, axis, down)
        array = jnp.concatenate([before, array, after], axis=dim)
    return array


def xor_pairs(size, mask):
    return [(i, i ^ mask) for i in range(size)]


def low_bits(size):
    bits = []
    bit = 1
    while bit < size:
        bits.append(bit)
        bit *= 2
    return bits


def pack(terms, rows_of):
    flat = jnp.concatenate([t.reshape(-1) for t in terms])
    total = flat.shape[0]
    rows = rows_of(-(-total // 128))
    return jnp.pad(flat, (0, rows * 128 - total)).reshape(rows, 128)


def unpack(flat, terms):
    flat = flat.reshape(-1)
    out = []
    offset = 0
    for t in terms:
        out.append(flat[offset : offset + t.size].reshape(t.shape))
        offset += t.size
    return out


def tree_psum(terms, late_fn, late_inputs):
    strip_bits = low_bits(lax.axis_size("strip"))
    slide_bits = low_bits(lax.axis_size("slide"))
    scatter = [("strip", b) for b in strip_bits[:2]]
    stages = [("slide", slide_bits[i : i + 2]) for i in range(0, len(slide_bits), 2)]
    stages += [("strip", [b]) for b in strip_bits[2:]]
    pieces = 2 ** len(scatter)
    main = pack(terms, lambda r: -(-r // (8 * pieces)) * 8 * pieces)
    main = main.reshape(pieces, -1, 128)
    for axis, bit in scatter:
        size = lax.axis_size(axis)
        half = main.shape[0] // 2
        mine = (lax.axis_index(axis) // bit) % 2
        keep = lax.dynamic_slice_in_dim(main, mine * half, half, axis=0)
        give = lax.dynamic_slice_in_dim(main, (1 - mine) * half, half, axis=0)
        main = keep + lax.ppermute(give, axis, xor_pairs(size, bit))
        if late_inputs is not None:
            main, late_inputs = lax.optimization_barrier((main, late_inputs))
            late_terms = late_fn(*late_inputs)
            late_inputs = None
    piece_rows = main.shape[1]
    late = pack(late_terms, lambda r: -(-r // 8) * 8)
    both = jnp.concatenate([main.reshape(-1, 128), late], axis=0)
    for axis, bits in stages:
        size = lax.axis_size(axis)
        masks = []
        for m in range(1, 2 ** len(bits)):
            masks.append(sum(b for k, b in enumerate(bits) if (m >> k) & 1))
        got = [lax.ppermute(both, axis, xor_pairs(size, mask)) for mask in masks]
        for item in got:
            both = both + item
    main = both[:piece_rows][None]
    late = both[piece_rows:]
    for axis, bit in reversed(scatter):
        size = lax.axis_size(axis)
        mine = (lax.axis_index(axis) // bit) % 2
        both = jnp.concatenate([main.reshape(-1, 128), late], axis=0)
        got = lax.ppermute(both, axis, xor_pairs(size, bit))
        cut = main.shape[0] * piece_rows
        theirs = got[:cut].reshape(main.shape)
        late = late + got[cut:]
        low = jnp.where(mine == 0, main, theirs)
        high = jnp.where(mine == 0, theirs, main)
        main = jnp.concatenate([low, high], axis=0)
    return unpack(main, terms), unpack(late, late_terms)


def gelu_slope(value):
    return 0.5 * (1.0 + jax.scipy.special.erf(value / math.sqrt(2.0))) + value * jnp.exp(
        -0.5 * value * value
    ) / math.sqrt(2.0 * math.pi)


def on_device(
    images,
    cotangent,
    conv_weight,
    conv_bias,
    norm_gain,
    norm_bias,
    up_weight,
    up_bias,
    down_weight,
    down_bias,
    layer_scale,
):
    slides_here = images.shape[0]
    chans = images.shape[1]
    rows = images.shape[2]
    cols = images.shape[3]
    kernel = conv_weight.shape[1]
    extended = with_halo(images, (("strip", 2),), 3)
    upstream = cotangent.astype(jnp.float32)
    padded = jnp.pad(extended, ((0, 0), (0, 0), (0, 0), (3, 3)))
    conv = jnp.zeros((slides_here, chans, rows, cols), jnp.float32) + conv_bias[None, :, None, None]
    for a in range(kernel):
        for b in range(kernel):
            conv = (
                conv
                + conv_weight[:, a, b][None, :, None, None]
                * padded[:, :, a : a + rows, b : b + cols]
            )
    centre = conv - jnp.mean(conv, axis=1, keepdims=True)
    inv = lax.rsqrt(jnp.mean(centre * centre, axis=1, keepdims=True) + 1e-06)
    normed = centre * inv
    lifted = (normed * norm_gain[None, :, None, None] + norm_bias[None, :, None, None]).astype(
        jnp.bfloat16
    )
    pre = (
        jnp.einsum("scrw,cf->sfrw", lifted, up_weight, preferred_element_type=jnp.float32)
        + up_bias[None, :, None, None]
    )
    act = jax.nn.gelu(pre, approximate=False).astype(jnp.bfloat16)
    branch = (
        jnp.einsum("sfrw,fc->scrw", act, down_weight, preferred_element_type=jnp.float32)
        + down_bias[None, :, None, None]
    )
    d_branch = (layer_scale[None, :, None, None] * upstream).astype(jnp.bfloat16)
    d_act = jnp.einsum("scrw,fc->sfrw", d_branch, down_weight, preferred_element_type=jnp.float32)
    d_pre = (d_act * gelu_slope(pre)).astype(jnp.bfloat16)
    d_lifted = jnp.einsum("sfrw,cf->scrw", d_pre, up_weight, preferred_element_type=jnp.float32)
    d_normed = d_lifted * norm_gain[None, :, None, None]
    d_conv = inv * (
        d_normed
        - jnp.mean(d_normed, axis=1, keepdims=True)
        - normed * jnp.mean(d_normed * normed, axis=1, keepdims=True)
    )
    d_wide = with_halo(d_conv, (("strip", 2),), 3)
    d_padded = jnp.pad(d_wide, ((0, 0), (0, 0), (0, 0), (3, 3)))
    image_grad = cotangent.astype(jnp.float32)
    for a in range(kernel):
        for b in range(kernel):
            image_grad = (
                image_grad
                + conv_weight[:, a, b][None, :, None, None]
                * d_padded[:, :, 6 - a : 6 - a + rows, 6 - b : 6 - b + cols]
            )
    pixel_count = slides_here * lax.axis_size("slide") * rows * lax.axis_size("strip") * cols
    scale = 1.0 / math.sqrt(float(pixel_count))

    def conv_terms(d_conv, padded):
        taps = []
        for a in range(kernel):
            for b in range(kernel):
                window = padded[:, :, a : a + rows, b : b + cols]
                taps.append(jnp.sum(d_conv * window, axis=(0, 2, 3)))
        return [jnp.stack(taps, axis=0) * scale, jnp.sum(d_conv, axis=(0, 2, 3)) * scale]

    terms = (
        jnp.einsum("scrw,sfrw->cf", lifted, d_pre, preferred_element_type=jnp.float32),
        jnp.einsum("scrw,sfrw->cf", d_branch, act, preferred_element_type=jnp.float32),
        jnp.sum(d_lifted * normed, axis=(0, 2, 3)),
        jnp.sum(d_lifted, axis=(0, 2, 3)),
        jnp.sum(d_pre.astype(jnp.float32), axis=(0, 2, 3)),
        jnp.sum(d_branch.astype(jnp.float32), axis=(0, 2, 3)),
        jnp.sum(upstream * branch, axis=(0, 2, 3)),
    )
    main, late = tree_psum([item * scale for item in terms], conv_terms, (d_conv, padded))
    g = [late[0].reshape(kernel, kernel, chans).transpose(2, 0, 1), late[1]]
    g += [main[2], main[3], main[0], main[4], main[1].T, main[5], main[6]]
    return (image_grad.astype(jnp.bfloat16), g[0], g[1], g[2], g[3], g[4], g[5], g[6], g[7], g[8])


def solution(mesh):
    in_specs = (
        P("slide", None, "strip", None),
        P("slide", None, "strip", None),
        P(),
        P(),
        P(),
        P(),
        P(),
        P(),
        P(),
        P(),
        P(),
    )
    out_specs = (P("slide", None, "strip", None), P(), P(), P(), P(), P(), P(), P(), P(), P())
    return jax.shard_map(
        on_device, mesh=mesh, in_specs=in_specs, out_specs=out_specs, check_vma=False
    )
```

```python
import math

import jax
import jax.numpy as jnp
from jax import lax
from jax.sharding import PartitionSpec as P


def with_halo(array, sides, width):
    for axis, dim in sides:
        size, length = (lax.axis_size(axis), array.shape[dim])
        up = [(i, (i + 1) % size) for i in range(size - 1)]
        down = [(j, i) for i, j in up]
        last = lax.slice_in_dim(array, length - width, length, axis=dim)
        first = lax.slice_in_dim(array, 0, width, axis=dim)
        before = lax.ppermute(last, axis, up)
        after = lax.ppermute(first, axis, down)
        array = jnp.concatenate([before, array, after], axis=dim)
    return array


def xor_pairs(size, mask):
    return [(i, i ^ mask) for i in range(size)]


def low_bits(size):
    bits = []
    bit = 1
    while bit < size:
        bits.append(bit)
        bit *= 2
    return bits


def tree_psum(terms):
    shapes = [t.shape for t in terms]
    sizes = [math.prod(s) for s in shapes]
    total = sum(sizes)
    strip_bits = low_bits(lax.axis_size("strip"))
    slide_bits = low_bits(lax.axis_size("slide"))
    scatter = [("strip", b) for b in strip_bits[:2]]
    stages = [("slide", slide_bits[i : i + 2]) for i in range(0, len(slide_bits), 2)]
    stages += [("strip", [b]) for b in strip_bits[2:]]
    pieces = 2 ** len(scatter)
    rows = -(-total // (pieces * 128))
    rows = -(-rows // 8) * 8
    order = sorted(range(len(terms)), key=lambda i: -sizes[i])
    flat = jnp.concatenate([terms[i].reshape(-1) for i in order])
    flat = jnp.pad(flat, (0, pieces * rows * 128 - total)).reshape(pieces, rows, 128)
    for axis, bit in scatter:
        size = lax.axis_size(axis)
        half = flat.shape[0] // 2
        mine = (lax.axis_index(axis) // bit) % 2
        keep = lax.dynamic_slice_in_dim(flat, mine * half, half, axis=0)
        give = lax.dynamic_slice_in_dim(flat, (1 - mine) * half, half, axis=0)
        flat = keep + lax.ppermute(give, axis, xor_pairs(size, bit))
    for axis, bits in stages:
        size = lax.axis_size(axis)
        masks = []
        for m in range(1, 2 ** len(bits)):
            masks.append(sum(b for k, b in enumerate(bits) if (m >> k) & 1))
        got = [lax.ppermute(flat, axis, xor_pairs(size, mask)) for mask in masks]
        for item in got:
            flat = flat + item
    flat = flat.astype(jnp.bfloat16)
    for axis, bit in reversed(scatter):
        size = lax.axis_size(axis)
        mine = (lax.axis_index(axis) // bit) % 2
        got = lax.ppermute(flat, axis, xor_pairs(size, bit))
        low = jnp.where(mine == 0, flat, got)
        high = jnp.where(mine == 0, got, flat)
        flat = jnp.concatenate([low, high], axis=0)
    flat = flat.reshape(-1)
    offset = 0
    out = [None] * len(terms)
    for i in order:
        out[i] = flat[offset : offset + sizes[i]].reshape(shapes[i]).astype(jnp.float32)
        offset += sizes[i]
    return out


def gelu_slope(value):
    return 0.5 * (1.0 + jax.scipy.special.erf(value / math.sqrt(2.0))) + value * jnp.exp(
        -0.5 * value * value
    ) / math.sqrt(2.0 * math.pi)


def on_device(
    images,
    cotangent,
    conv_weight,
    conv_bias,
    norm_gain,
    norm_bias,
    up_weight,
    up_bias,
    down_weight,
    down_bias,
    layer_scale,
):
    slides_here = images.shape[0]
    chans = images.shape[1]
    rows = images.shape[2]
    cols = images.shape[3]
    kernel = conv_weight.shape[1]
    extended = with_halo(images, (("strip", 2),), 3)
    upstream = cotangent.astype(jnp.float32)
    padded = jnp.pad(extended, ((0, 0), (0, 0), (0, 0), (3, 3)))
    conv = jnp.zeros((slides_here, chans, rows, cols), jnp.float32) + conv_bias[None, :, None, None]
    for a in range(kernel):
        for b in range(kernel):
            conv = (
                conv
                + conv_weight[:, a, b][None, :, None, None]
                * padded[:, :, a : a + rows, b : b + cols]
            )
    centre = conv - jnp.mean(conv, axis=1, keepdims=True)
    inv = lax.rsqrt(jnp.mean(centre * centre, axis=1, keepdims=True) + 1e-06)
    normed = centre * inv
    lifted = (normed * norm_gain[None, :, None, None] + norm_bias[None, :, None, None]).astype(
        jnp.bfloat16
    )
    pre = (
        jnp.einsum("scrw,cf->sfrw", lifted, up_weight, preferred_element_type=jnp.float32)
        + up_bias[None, :, None, None]
    )
    act = jax.nn.gelu(pre, approximate=False).astype(jnp.bfloat16)
    branch = (
        jnp.einsum("sfrw,fc->scrw", act, down_weight, preferred_element_type=jnp.float32)
        + down_bias[None, :, None, None]
    )
    d_branch = (layer_scale[None, :, None, None] * upstream).astype(jnp.bfloat16)
    d_act = jnp.einsum("scrw,fc->sfrw", d_branch, down_weight, preferred_element_type=jnp.float32)
    d_pre = (d_act * gelu_slope(pre)).astype(jnp.bfloat16)
    d_lifted = jnp.einsum("sfrw,cf->scrw", d_pre, up_weight, preferred_element_type=jnp.float32)
    d_normed = d_lifted * norm_gain[None, :, None, None]
    d_conv = inv * (
        d_normed
        - jnp.mean(d_normed, axis=1, keepdims=True)
        - normed * jnp.mean(d_normed * normed, axis=1, keepdims=True)
    )
    d_wide = with_halo(d_conv, (("strip", 2),), 3)
    d_padded = jnp.pad(d_wide, ((0, 0), (0, 0), (0, 0), (3, 3)))
    image_grad = cotangent.astype(jnp.float32)
    taps = []
    for a in range(kernel):
        for b in range(kernel):
            image_grad = (
                image_grad
                + conv_weight[:, a, b][None, :, None, None]
                * d_padded[:, :, 6 - a : 6 - a + rows, 6 - b : 6 - b + cols]
            )
            taps.append(jnp.sum(d_conv * padded[:, :, a : a + rows, b : b + cols], axis=(0, 2, 3)))
    pixel_count = slides_here * lax.axis_size("slide") * rows * lax.axis_size("strip") * cols
    scale = 1.0 / math.sqrt(float(pixel_count))
    terms = (
        jnp.stack(taps, axis=0),
        jnp.sum(d_conv, axis=(0, 2, 3)),
        jnp.sum(d_lifted * normed, axis=(0, 2, 3)),
        jnp.sum(d_lifted, axis=(0, 2, 3)),
        jnp.einsum("scrw,sfrw->cf", lifted, d_pre, preferred_element_type=jnp.float32),
        jnp.sum(d_pre.astype(jnp.float32), axis=(0, 2, 3)),
        jnp.einsum("scrw,sfrw->cf", d_branch, act, preferred_element_type=jnp.float32),
        jnp.sum(d_branch.astype(jnp.float32), axis=(0, 2, 3)),
        jnp.sum(upstream * branch, axis=(0, 2, 3)),
    )
    g = tree_psum([item * scale for item in terms])
    g[0] = g[0].reshape(kernel, kernel, chans).transpose(2, 0, 1)
    g[6] = g[6].T
    return (image_grad.astype(jnp.bfloat16), g[0], g[1], g[2], g[3], g[4], g[5], g[6], g[7], g[8])


def solution(mesh):
    in_specs = (
        P("slide", None, "strip", None),
        P("slide", None, "strip", None),
        P(),
        P(),
        P(),
        P(),
        P(),
        P(),
        P(),
        P(),
        P(),
    )
    out_specs = (P("slide", None, "strip", None), P(), P(), P(), P(), P(), P(), P(), P(), P())
    return jax.shard_map(
        on_device, mesh=mesh, in_specs=in_specs, out_specs=out_specs, check_vma=False
    )
```

```python
import math

import jax
import jax.numpy as jnp
from jax import lax
from jax.sharding import PartitionSpec as P


def with_halo(array, sides, width):
    for axis, dim in sides:
        size, length = (lax.axis_size(axis), array.shape[dim])
        up = [(i, (i + 1) % size) for i in range(size - 1)]
        down = [(j, i) for i, j in up]
        last = lax.slice_in_dim(array, length - width, length, axis=dim)
        first = lax.slice_in_dim(array, 0, width, axis=dim)
        before = lax.ppermute(last, axis, up)
        after = lax.ppermute(first, axis, down)
        array = jnp.concatenate([before, array, after], axis=dim)
    return array


def xor_pairs(size, mask):
    return [(i, i ^ mask) for i in range(size)]


def low_bits(size):
    bits = []
    bit = 1
    while bit < size:
        bits.append(bit)
        bit *= 2
    return bits


def tree_psum(terms, hold):
    shapes = [t.shape for t in terms]
    sizes = [math.prod(s) for s in shapes]
    rooms = [-(-size // 1024) * 1024 for size in sizes]
    total = sum(rooms)
    strip_bits = low_bits(lax.axis_size("strip"))
    slide_bits = low_bits(lax.axis_size("slide"))
    scatter = [("strip", b) for b in strip_bits[:2]]
    stages = [("slide", slide_bits[i : i + 2]) for i in range(0, len(slide_bits), 2)]
    stages += [("strip", [b]) for b in strip_bits[2:]]
    pieces = 2 ** len(scatter)
    rows = -(-total // (pieces * 128))
    rows = -(-rows // 8) * 8
    flat = jnp.concatenate([jnp.pad(t.reshape(-1), (0, room - size)) for t, size, room in zip(terms, sizes, rooms)])
    flat = jnp.pad(flat, (0, pieces * rows * 128 - total)).reshape(pieces, rows, 128)
    for axis, bit in scatter:
        size = lax.axis_size(axis)
        half = flat.shape[0] // 2
        mine = (lax.axis_index(axis) // bit) % 2
        keep = lax.dynamic_slice_in_dim(flat, mine * half, half, axis=0)
        give = lax.dynamic_slice_in_dim(flat, (1 - mine) * half, half, axis=0)
        flat = keep + lax.ppermute(give, axis, xor_pairs(size, bit))
    for axis, bits in stages:
        size = lax.axis_size(axis)
        masks = []
        for m in range(1, 2 ** len(bits)):
            masks.append(sum(b for k, b in enumerate(bits) if (m >> k) & 1))
        got = [lax.ppermute(flat, axis, xor_pairs(size, mask)) for mask in masks]
        for item in got:
            flat = flat + item
    flat, hold = lax.optimization_barrier((flat, hold))
    for axis, bit in reversed(scatter):
        size = lax.axis_size(axis)
        mine = (lax.axis_index(axis) // bit) % 2
        got = lax.ppermute(flat, axis, xor_pairs(size, bit))
        low = jnp.where(mine == 0, flat, got)
        high = jnp.where(mine == 0, got, flat)
        flat = jnp.concatenate([low, high], axis=0)
    flat = flat.reshape(-1)
    out = []
    offset = 0
    for shape, size, room in zip(shapes, sizes, rooms):
        out.append(flat[offset : offset + size].reshape(shape))
        offset += room
    return out, hold


def gelu_slope(value):
    return 0.5 * (1.0 + jax.scipy.special.erf(value / math.sqrt(2.0))) + value * jnp.exp(
        -0.5 * value * value
    ) / math.sqrt(2.0 * math.pi)


def on_device(
    images,
    cotangent,
    conv_weight,
    conv_bias,
    norm_gain,
    norm_bias,
    up_weight,
    up_bias,
    down_weight,
    down_bias,
    layer_scale,
):
    slides_here = images.shape[0]
    chans = images.shape[1]
    rows = images.shape[2]
    cols = images.shape[3]
    kernel = conv_weight.shape[1]
    extended = with_halo(images, (("strip", 2),), 3)
    upstream = cotangent.astype(jnp.float32)
    padded = jnp.pad(extended, ((0, 0), (0, 0), (0, 0), (3, 3)))
    conv = jnp.zeros((slides_here, chans, rows, cols), jnp.float32) + conv_bias[None, :, None, None]
    for a in range(kernel):
        for b in range(kernel):
            conv = (
                conv
                + conv_weight[:, a, b][None, :, None, None]
                * padded[:, :, a : a + rows, b : b + cols]
            )
    centre = conv - jnp.mean(conv, axis=1, keepdims=True)
    inv = lax.rsqrt(jnp.mean(centre * centre, axis=1, keepdims=True) + 1e-06)
    normed = centre * inv
    lifted = (normed * norm_gain[None, :, None, None] + norm_bias[None, :, None, None]).astype(
        jnp.bfloat16
    )
    pre = (
        jnp.einsum("scrw,cf->sfrw", lifted, up_weight, preferred_element_type=jnp.float32)
        + up_bias[None, :, None, None]
    )
    act = jax.nn.gelu(pre, approximate=False).astype(jnp.bfloat16)
    branch = (
        jnp.einsum("sfrw,fc->scrw", act, down_weight, preferred_element_type=jnp.float32)
        + down_bias[None, :, None, None]
    )
    d_branch = (layer_scale[None, :, None, None] * upstream).astype(jnp.bfloat16)
    d_act = jnp.einsum("scrw,fc->sfrw", d_branch, down_weight, preferred_element_type=jnp.float32)
    d_pre = (d_act * gelu_slope(pre)).astype(jnp.bfloat16)
    d_lifted = jnp.einsum("sfrw,cf->scrw", d_pre, up_weight, preferred_element_type=jnp.float32)
    d_normed = d_lifted * norm_gain[None, :, None, None]
    d_conv = inv * (
        d_normed
        - jnp.mean(d_normed, axis=1, keepdims=True)
        - normed * jnp.mean(d_normed * normed, axis=1, keepdims=True)
    )
    d_wide = with_halo(d_conv, (("strip", 2),), 3)
    d_padded = jnp.pad(d_wide, ((0, 0), (0, 0), (0, 0), (3, 3)))
    image_grad = cotangent.astype(jnp.float32)
    taps = []
    for a in range(kernel):
        for b in range(kernel):
            image_grad = (
                image_grad
                + conv_weight[:, a, b][None, :, None, None]
                * d_padded[:, :, 6 - a : 6 - a + rows, 6 - b : 6 - b + cols]
            )
            taps.append(jnp.sum(d_conv * padded[:, :, a : a + rows, b : b + cols], axis=(0, 2, 3)))
    pixel_count = slides_here * lax.axis_size("slide") * rows * lax.axis_size("strip") * cols
    scale = 1.0 / math.sqrt(float(pixel_count))
    terms = (
        jnp.stack(taps, axis=0),
        jnp.sum(d_conv, axis=(0, 2, 3)),
        jnp.sum(d_lifted * normed, axis=(0, 2, 3)),
        jnp.sum(d_lifted, axis=(0, 2, 3)),
        jnp.einsum("scrw,sfrw->cf", lifted, d_pre, preferred_element_type=jnp.float32),
        jnp.sum(d_pre.astype(jnp.float32), axis=(0, 2, 3)),
        jnp.einsum("scrw,sfrw->cf", d_branch, act, preferred_element_type=jnp.float32),
        jnp.sum(d_branch.astype(jnp.float32), axis=(0, 2, 3)),
        jnp.sum(upstream * branch, axis=(0, 2, 3)),
    )
    g, image_grad = tree_psum([item * scale for item in terms], image_grad.astype(jnp.bfloat16))
    g[0] = g[0].reshape(kernel, kernel, chans).transpose(2, 0, 1)
    g[6] = g[6].T
    return (image_grad, g[0], g[1], g[2], g[3], g[4], g[5], g[6], g[7], g[8])


def solution(mesh):
    in_specs = (
        P("slide", None, "strip", None),
        P("slide", None, "strip", None),
        P(),
        P(),
        P(),
        P(),
        P(),
        P(),
        P(),
        P(),
        P(),
    )
    out_specs = (P("slide", None, "strip", None), P(), P(), P(), P(), P(), P(), P(), P(), P())
    return jax.shard_map(
        on_device, mesh=mesh, in_specs=in_specs, out_specs=out_specs, check_vma=False
    )
```

```python
import math

import jax
import jax.numpy as jnp
from jax import lax
from jax.sharding import PartitionSpec as P


def with_halo(array, sides, width, whole=False):
    for axis, dim in sides:
        size, length = (lax.axis_size(axis), array.shape[dim])
        up = [(i, (i + 1) % size) for i in range(size - 1)]
        down = [(j, i) for i, j in up]
        if whole:
            before = lax.ppermute(array, axis, up)
            after = lax.ppermute(array, axis, down)
            before = lax.slice_in_dim(before, length - width, length, axis=dim)
            after = lax.slice_in_dim(after, 0, width, axis=dim)
            array = jnp.concatenate([before, array, after], axis=dim)
            continue
        last = lax.slice_in_dim(array, length - width, length, axis=dim)
        first = lax.slice_in_dim(array, 0, width, axis=dim)
        before = lax.ppermute(last, axis, up)
        after = lax.ppermute(first, axis, down)
        array = jnp.concatenate([before, array, after], axis=dim)
    return array


def xor_pairs(size, mask):
    return [(i, i ^ mask) for i in range(size)]


def low_bits(size):
    bits = []
    bit = 1
    while bit < size:
        bits.append(bit)
        bit *= 2
    return bits


def tree_psum(terms, hold):
    shapes = [t.shape for t in terms]
    sizes = [math.prod(s) for s in shapes]
    rooms = [-(-size // 1024) * 1024 for size in sizes]
    total = sum(rooms)
    strip_bits = low_bits(lax.axis_size("strip"))
    slide_bits = low_bits(lax.axis_size("slide"))
    scatter = [("strip", b) for b in strip_bits[:2]]
    stages = [("slide", slide_bits[i : i + 2]) for i in range(0, len(slide_bits), 2)]
    stages += [("strip", [b]) for b in strip_bits[2:]]
    pieces = 2 ** len(scatter)
    rows = -(-total // (pieces * 128))
    rows = -(-rows // 8) * 8
    flat = jnp.concatenate([jnp.pad(t.reshape(-1), (0, room - size)) for t, size, room in zip(terms, sizes, rooms)])
    flat = jnp.pad(flat, (0, pieces * rows * 128 - total)).reshape(pieces, rows, 128)
    for axis, bit in scatter:
        size = lax.axis_size(axis)
        half = flat.shape[0] // 2
        mine = (lax.axis_index(axis) // bit) % 2
        keep = lax.dynamic_slice_in_dim(flat, mine * half, half, axis=0)
        give = lax.dynamic_slice_in_dim(flat, (1 - mine) * half, half, axis=0)
        flat = keep + lax.ppermute(give, axis, xor_pairs(size, bit))
    for axis, bits in stages:
        size = lax.axis_size(axis)
        masks = []
        for m in range(1, 2 ** len(bits)):
            masks.append(sum(b for k, b in enumerate(bits) if (m >> k) & 1))
        got = [lax.ppermute(flat, axis, xor_pairs(size, mask)) for mask in masks]
        for item in got:
            flat = flat + item
    flat, hold = lax.optimization_barrier((flat, hold))
    for axis, bit in reversed(scatter):
        size = lax.axis_size(axis)
        mine = (lax.axis_index(axis) // bit) % 2
        got = lax.ppermute(flat, axis, xor_pairs(size, bit))
        low = jnp.where(mine == 0, flat, got)
        high = jnp.where(mine == 0, got, flat)
        flat = jnp.concatenate([low, high], axis=0)
    flat = flat.reshape(-1)
    out = []
    offset = 0
    for shape, size, room in zip(shapes, sizes, rooms):
        out.append(flat[offset : offset + size].reshape(shape))
        offset += room
    return out, hold


def gelu_slope(value):
    return 0.5 * (1.0 + jax.scipy.special.erf(value / math.sqrt(2.0))) + value * jnp.exp(
        -0.5 * value * value
    ) / math.sqrt(2.0 * math.pi)


def on_device(
    images,
    cotangent,
    conv_weight,
    conv_bias,
    norm_gain,
    norm_bias,
    up_weight,
    up_bias,
    down_weight,
    down_bias,
    layer_scale,
):
    slides_here = images.shape[0]
    chans = images.shape[1]
    rows = images.shape[2]
    cols = images.shape[3]
    kernel = conv_weight.shape[1]
    extended = with_halo(images, (("strip", 2),), 3, whole=True)
    upstream = cotangent.astype(jnp.float32)
    padded = jnp.pad(extended, ((0, 0), (0, 0), (0, 0), (3, 3)))
    conv = jnp.zeros((slides_here, chans, rows, cols), jnp.float32) + conv_bias[None, :, None, None]
    for a in range(kernel):
        for b in range(kernel):
            conv = (
                conv
                + conv_weight[:, a, b][None, :, None, None]
                * padded[:, :, a : a + rows, b : b + cols]
            )
    centre = conv - jnp.mean(conv, axis=1, keepdims=True)
    inv = lax.rsqrt(jnp.mean(centre * centre, axis=1, keepdims=True) + 1e-06)
    normed = centre * inv
    lifted = (normed * norm_gain[None, :, None, None] + norm_bias[None, :, None, None]).astype(
        jnp.bfloat16
    )
    pre = (
        jnp.einsum("scrw,cf->sfrw", lifted, up_weight, preferred_element_type=jnp.float32)
        + up_bias[None, :, None, None]
    )
    act = jax.nn.gelu(pre, approximate=False).astype(jnp.bfloat16)
    branch = (
        jnp.einsum("sfrw,fc->scrw", act, down_weight, preferred_element_type=jnp.float32)
        + down_bias[None, :, None, None]
    )
    d_branch = (layer_scale[None, :, None, None] * upstream).astype(jnp.bfloat16)
    d_act = jnp.einsum("scrw,fc->sfrw", d_branch, down_weight, preferred_element_type=jnp.float32)
    d_pre = (d_act * gelu_slope(pre)).astype(jnp.bfloat16)
    d_lifted = jnp.einsum("sfrw,cf->scrw", d_pre, up_weight, preferred_element_type=jnp.float32)
    d_normed = d_lifted * norm_gain[None, :, None, None]
    d_conv = inv * (
        d_normed
        - jnp.mean(d_normed, axis=1, keepdims=True)
        - normed * jnp.mean(d_normed * normed, axis=1, keepdims=True)
    )
    d_wide = with_halo(d_conv, (("strip", 2),), 3)
    d_padded = jnp.pad(d_wide, ((0, 0), (0, 0), (0, 0), (3, 3)))
    image_grad = cotangent.astype(jnp.float32)
    taps = []
    for a in range(kernel):
        for b in range(kernel):
            image_grad = (
                image_grad
                + conv_weight[:, a, b][None, :, None, None]
                * d_padded[:, :, 6 - a : 6 - a + rows, 6 - b : 6 - b + cols]
            )
            taps.append(jnp.sum(d_conv * padded[:, :, a : a + rows, b : b + cols], axis=(0, 2, 3)))
    pixel_count = slides_here * lax.axis_size("slide") * rows * lax.axis_size("strip") * cols
    scale = 1.0 / math.sqrt(float(pixel_count))
    terms = (
        jnp.stack(taps, axis=0),
        jnp.sum(d_conv, axis=(0, 2, 3)),
        jnp.sum(d_lifted * normed, axis=(0, 2, 3)),
        jnp.sum(d_lifted, axis=(0, 2, 3)),
        jnp.einsum("scrw,sfrw->cf", lifted, d_pre, preferred_element_type=jnp.float32),
        jnp.sum(d_pre.astype(jnp.float32), axis=(0, 2, 3)),
        jnp.einsum("scrw,sfrw->cf", d_branch, act, preferred_element_type=jnp.float32),
        jnp.sum(d_branch.astype(jnp.float32), axis=(0, 2, 3)),
        jnp.sum(upstream * branch, axis=(0, 2, 3)),
    )
    g, image_grad = tree_psum([item * scale for item in terms], image_grad.astype(jnp.bfloat16))
    g[0] = g[0].reshape(kernel, kernel, chans).transpose(2, 0, 1)
    g[6] = g[6].T
    return (image_grad, g[0], g[1], g[2], g[3], g[4], g[5], g[6], g[7], g[8])


def solution(mesh):
    in_specs = (
        P("slide", None, "strip", None),
        P("slide", None, "strip", None),
        P(),
        P(),
        P(),
        P(),
        P(),
        P(),
        P(),
        P(),
        P(),
    )
    out_specs = (P("slide", None, "strip", None), P(), P(), P(), P(), P(), P(), P(), P(), P())
    return jax.shard_map(
        on_device, mesh=mesh, in_specs=in_specs, out_specs=out_specs, check_vma=False
    )
```

```python
import math

import jax
import jax.numpy as jnp
from jax import lax
from jax.sharding import PartitionSpec as P


def with_halo(array, sides, width, whole=False):
    for axis, dim in sides:
        size, length = (lax.axis_size(axis), array.shape[dim])
        up = [(i, (i + 1) % size) for i in range(size - 1)]
        down = [(j, i) for i, j in up]
        if whole:
            before = lax.ppermute(array, axis, up)
            after = lax.ppermute(array, axis, down)
            before = lax.slice_in_dim(before, length - width, length, axis=dim)
            after = lax.slice_in_dim(after, 0, width, axis=dim)
            array = jnp.concatenate([before, array, after], axis=dim)
            continue
        last = lax.slice_in_dim(array, length - width, length, axis=dim)
        first = lax.slice_in_dim(array, 0, width, axis=dim)
        before = lax.ppermute(last, axis, up)
        after = lax.ppermute(first, axis, down)
        array = jnp.concatenate([before, array, after], axis=dim)
    return array


def xor_pairs(size, mask):
    return [(i, i ^ mask) for i in range(size)]


def low_bits(size):
    bits = []
    bit = 1
    while bit < size:
        bits.append(bit)
        bit *= 2
    return bits


def tree_psum(terms, side_fn, side_in):
    shapes = [t.shape for t in terms]
    sizes = [math.prod(s) for s in shapes]
    rooms = [-(-size // 1024) * 1024 for size in sizes]
    total = sum(rooms)
    strip_bits = low_bits(lax.axis_size("strip"))
    slide_bits = low_bits(lax.axis_size("slide"))
    scatter = [("strip", b) for b in strip_bits[:2]]
    stages = [("slide", slide_bits[i : i + 2]) for i in range(0, len(slide_bits), 2)]
    stages += [("strip", [b]) for b in strip_bits[2:]]
    pieces = 2 ** len(scatter)
    rows = -(-total // (pieces * 128))
    rows = -(-rows // 8) * 8
    flat = jnp.concatenate([jnp.pad(t.reshape(-1), (0, room - size)) for t, size, room in zip(terms, sizes, rooms)])
    flat = jnp.pad(flat, (0, pieces * rows * 128 - total)).reshape(pieces, rows, 128)
    for axis, bit in scatter:
        size = lax.axis_size(axis)
        half = flat.shape[0] // 2
        mine = (lax.axis_index(axis) // bit) % 2
        keep = lax.dynamic_slice_in_dim(flat, mine * half, half, axis=0)
        give = lax.dynamic_slice_in_dim(flat, (1 - mine) * half, half, axis=0)
        flat = keep + lax.ppermute(give, axis, xor_pairs(size, bit))
    flat, side_in = lax.optimization_barrier((flat, side_in))
    hold = side_fn(*side_in)
    for axis, bits in stages:
        size = lax.axis_size(axis)
        masks = []
        for m in range(1, 2 ** len(bits)):
            masks.append(sum(b for k, b in enumerate(bits) if (m >> k) & 1))
        got = [lax.ppermute(flat, axis, xor_pairs(size, mask)) for mask in masks]
        for item in got:
            flat = flat + item
    flat, hold = lax.optimization_barrier((flat, hold))
    for axis, bit in reversed(scatter):
        size = lax.axis_size(axis)
        mine = (lax.axis_index(axis) // bit) % 2
        got = lax.ppermute(flat, axis, xor_pairs(size, bit))
        low = jnp.where(mine == 0, flat, got)
        high = jnp.where(mine == 0, got, flat)
        flat = jnp.concatenate([low, high], axis=0)
    flat = flat.reshape(-1)
    out = []
    offset = 0
    for shape, size, room in zip(shapes, sizes, rooms):
        out.append(flat[offset : offset + size].reshape(shape))
        offset += room
    return out, hold


def gelu_slope(value):
    return 0.5 * (1.0 + jax.scipy.special.erf(value / math.sqrt(2.0))) + value * jnp.exp(
        -0.5 * value * value
    ) / math.sqrt(2.0 * math.pi)


def on_device(
    images,
    cotangent,
    conv_weight,
    conv_bias,
    norm_gain,
    norm_bias,
    up_weight,
    up_bias,
    down_weight,
    down_bias,
    layer_scale,
):
    slides_here = images.shape[0]
    chans = images.shape[1]
    rows = images.shape[2]
    cols = images.shape[3]
    kernel = conv_weight.shape[1]
    extended = with_halo(images, (("strip", 2),), 3, whole=True)
    upstream = cotangent.astype(jnp.float32)
    padded = jnp.pad(extended, ((0, 0), (0, 0), (0, 0), (3, 3)))
    conv = jnp.zeros((slides_here, chans, rows, cols), jnp.float32) + conv_bias[None, :, None, None]
    for a in range(kernel):
        for b in range(kernel):
            conv = (
                conv
                + conv_weight[:, a, b][None, :, None, None]
                * padded[:, :, a : a + rows, b : b + cols]
            )
    centre = conv - jnp.mean(conv, axis=1, keepdims=True)
    inv = lax.rsqrt(jnp.mean(centre * centre, axis=1, keepdims=True) + 1e-06)
    normed = centre * inv
    lifted = (normed * norm_gain[None, :, None, None] + norm_bias[None, :, None, None]).astype(
        jnp.bfloat16
    )
    pre = (
        jnp.einsum("scrw,cf->sfrw", lifted, up_weight, preferred_element_type=jnp.float32)
        + up_bias[None, :, None, None]
    )
    act = jax.nn.gelu(pre, approximate=False).astype(jnp.bfloat16)
    branch = (
        jnp.einsum("sfrw,fc->scrw", act, down_weight, preferred_element_type=jnp.float32)
        + down_bias[None, :, None, None]
    )
    d_branch = (layer_scale[None, :, None, None] * upstream).astype(jnp.bfloat16)
    d_act = jnp.einsum("scrw,fc->sfrw", d_branch, down_weight, preferred_element_type=jnp.float32)
    d_pre = (d_act * gelu_slope(pre)).astype(jnp.bfloat16)
    d_lifted = jnp.einsum("sfrw,cf->scrw", d_pre, up_weight, preferred_element_type=jnp.float32)
    d_normed = d_lifted * norm_gain[None, :, None, None]
    d_conv = inv * (
        d_normed
        - jnp.mean(d_normed, axis=1, keepdims=True)
        - normed * jnp.mean(d_normed * normed, axis=1, keepdims=True)
    )
    def image_grad_of(d_conv, cotangent):
        d_wide = with_halo(d_conv, (("strip", 2),), 3)
        d_padded = jnp.pad(d_wide, ((0, 0), (0, 0), (0, 0), (3, 3)))
        image_grad = cotangent.astype(jnp.float32)
        for a in range(kernel):
            for b in range(kernel):
                image_grad = (
                    image_grad
                    + conv_weight[:, a, b][None, :, None, None]
                    * d_padded[:, :, 6 - a : 6 - a + rows, 6 - b : 6 - b + cols]
                )
        return image_grad.astype(jnp.bfloat16)

    taps = []
    for a in range(kernel):
        for b in range(kernel):
            taps.append(jnp.sum(d_conv * padded[:, :, a : a + rows, b : b + cols], axis=(0, 2, 3)))
    pixel_count = slides_here * lax.axis_size("slide") * rows * lax.axis_size("strip") * cols
    scale = 1.0 / math.sqrt(float(pixel_count))
    terms = (
        jnp.stack(taps, axis=0),
        jnp.sum(d_conv, axis=(0, 2, 3)),
        jnp.sum(d_lifted * normed, axis=(0, 2, 3)),
        jnp.sum(d_lifted, axis=(0, 2, 3)),
        jnp.einsum("scrw,sfrw->cf", lifted, d_pre, preferred_element_type=jnp.float32),
        jnp.sum(d_pre.astype(jnp.float32), axis=(0, 2, 3)),
        jnp.einsum("scrw,sfrw->cf", d_branch, act, preferred_element_type=jnp.float32),
        jnp.sum(d_branch.astype(jnp.float32), axis=(0, 2, 3)),
        jnp.sum(upstream * branch, axis=(0, 2, 3)),
    )
    g, image_grad = tree_psum(
        [item * scale for item in terms], image_grad_of, (d_conv, cotangent)
    )
    g[0] = g[0].reshape(kernel, kernel, chans).transpose(2, 0, 1)
    g[6] = g[6].T
    return (image_grad, g[0], g[1], g[2], g[3], g[4], g[5], g[6], g[7], g[8])


def solution(mesh):
    in_specs = (
        P("slide", None, "strip", None),
        P("slide", None, "strip", None),
        P(),
        P(),
        P(),
        P(),
        P(),
        P(),
        P(),
        P(),
        P(),
    )
    out_specs = (P("slide", None, "strip", None), P(), P(), P(), P(), P(), P(), P(), P(), P())
    return jax.shard_map(
        on_device, mesh=mesh, in_specs=in_specs, out_specs=out_specs, check_vma=False
    )
```

```python
import math

import jax
import jax.numpy as jnp
from jax import lax
from jax.sharding import PartitionSpec as P


def with_halo(array, sides, width, whole=False):
    for axis, dim in sides:
        size, length = (lax.axis_size(axis), array.shape[dim])
        up = [(i, (i + 1) % size) for i in range(size - 1)]
        down = [(j, i) for i, j in up]
        if whole:
            before = lax.ppermute(array, axis, up)
            after = lax.ppermute(array, axis, down)
            before = lax.slice_in_dim(before, length - width, length, axis=dim)
            after = lax.slice_in_dim(after, 0, width, axis=dim)
            array = jnp.concatenate([before, array, after], axis=dim)
            continue
        last = lax.slice_in_dim(array, length - width, length, axis=dim)
        first = lax.slice_in_dim(array, 0, width, axis=dim)
        before = lax.ppermute(last, axis, up)
        after = lax.ppermute(first, axis, down)
        array = jnp.concatenate([before, array, after], axis=dim)
    return array


def xor_pairs(size, mask):
    return [(i, i ^ mask) for i in range(size)]


def low_bits(size):
    bits = []
    bit = 1
    while bit < size:
        bits.append(bit)
        bit *= 2
    return bits


def tree_psum(terms, side_fn, side_in):
    shapes = [t.shape for t in terms]
    sizes = [math.prod(s) for s in shapes]
    rooms = [-(-size // 1024) * 1024 for size in sizes]
    total = sum(rooms)
    strip_bits = low_bits(lax.axis_size("strip"))
    slide_bits = low_bits(lax.axis_size("slide"))
    scatter = [("strip", b) for b in strip_bits[:2]]
    stages = [("slide", slide_bits[i : i + 2]) for i in range(0, len(slide_bits), 2)]
    stages += [("strip", [b]) for b in strip_bits[2:]]
    pieces = 2 ** len(scatter)
    rows = -(-total // (pieces * 128))
    rows = -(-rows // 8) * 8
    flat = jnp.concatenate([jnp.pad(t.reshape(-1), (0, room - size)) for t, size, room in zip(terms, sizes, rooms)])
    flat = jnp.pad(flat, (0, pieces * rows * 128 - total)).reshape(pieces, rows, 128)
    for axis, bit in scatter:
        size = lax.axis_size(axis)
        half = flat.shape[0] // 2
        mine = (lax.axis_index(axis) // bit) % 2
        keep = lax.dynamic_slice_in_dim(flat, mine * half, half, axis=0)
        give = lax.dynamic_slice_in_dim(flat, (1 - mine) * half, half, axis=0)
        flat = keep + lax.ppermute(give, axis, xor_pairs(size, bit))
    for axis, bits in stages:
        size = lax.axis_size(axis)
        masks = []
        for m in range(1, 2 ** len(bits)):
            masks.append(sum(b for k, b in enumerate(bits) if (m >> k) & 1))
        got = [lax.ppermute(flat, axis, xor_pairs(size, mask)) for mask in masks]
        for item in got:
            flat = flat + item
    flat, side_in = lax.optimization_barrier((flat, side_in))
    hold = side_fn(*side_in)
    for step, (axis, bit) in enumerate(reversed(scatter)):
        if step == len(scatter) - 1:
            flat, hold = lax.optimization_barrier((flat, hold))
        size = lax.axis_size(axis)
        mine = (lax.axis_index(axis) // bit) % 2
        got = lax.ppermute(flat, axis, xor_pairs(size, bit))
        low = jnp.where(mine == 0, flat, got)
        high = jnp.where(mine == 0, got, flat)
        flat = jnp.concatenate([low, high], axis=0)
    flat = flat.reshape(-1)
    out = []
    offset = 0
    for shape, size, room in zip(shapes, sizes, rooms):
        out.append(flat[offset : offset + size].reshape(shape))
        offset += room
    return out, hold


def gelu_slope(value):
    return 0.5 * (1.0 + jax.scipy.special.erf(value / math.sqrt(2.0))) + value * jnp.exp(
        -0.5 * value * value
    ) / math.sqrt(2.0 * math.pi)


def on_device(
    images,
    cotangent,
    conv_weight,
    conv_bias,
    norm_gain,
    norm_bias,
    up_weight,
    up_bias,
    down_weight,
    down_bias,
    layer_scale,
):
    slides_here = images.shape[0]
    chans = images.shape[1]
    rows = images.shape[2]
    cols = images.shape[3]
    kernel = conv_weight.shape[1]
    extended = with_halo(images, (("strip", 2),), 3, whole=True)
    upstream = cotangent.astype(jnp.float32)
    padded = jnp.pad(extended, ((0, 0), (0, 0), (0, 0), (3, 3)))
    conv = jnp.zeros((slides_here, chans, rows, cols), jnp.float32) + conv_bias[None, :, None, None]
    for a in range(kernel):
        for b in range(kernel):
            conv = (
                conv
                + conv_weight[:, a, b][None, :, None, None]
                * padded[:, :, a : a + rows, b : b + cols]
            )
    centre = conv - jnp.mean(conv, axis=1, keepdims=True)
    inv = lax.rsqrt(jnp.mean(centre * centre, axis=1, keepdims=True) + 1e-06)
    normed = centre * inv
    lifted = (normed * norm_gain[None, :, None, None] + norm_bias[None, :, None, None]).astype(
        jnp.bfloat16
    )
    pre = (
        jnp.einsum("scrw,cf->sfrw", lifted, up_weight, preferred_element_type=jnp.float32)
        + up_bias[None, :, None, None]
    )
    act = jax.nn.gelu(pre, approximate=False).astype(jnp.bfloat16)
    branch = (
        jnp.einsum("sfrw,fc->scrw", act, down_weight, preferred_element_type=jnp.float32)
        + down_bias[None, :, None, None]
    )
    d_branch = (layer_scale[None, :, None, None] * upstream).astype(jnp.bfloat16)
    d_act = jnp.einsum("scrw,fc->sfrw", d_branch, down_weight, preferred_element_type=jnp.float32)
    d_pre = (d_act * gelu_slope(pre)).astype(jnp.bfloat16)
    d_lifted = jnp.einsum("sfrw,cf->scrw", d_pre, up_weight, preferred_element_type=jnp.float32)
    d_normed = d_lifted * norm_gain[None, :, None, None]
    d_conv = inv * (
        d_normed
        - jnp.mean(d_normed, axis=1, keepdims=True)
        - normed * jnp.mean(d_normed * normed, axis=1, keepdims=True)
    )
    d_wide = with_halo(d_conv, (("strip", 2),), 3)
    d_padded = jnp.pad(d_wide, ((0, 0), (0, 0), (0, 0), (3, 3)))
    def image_grad_of(d_padded, cotangent):
        image_grad = cotangent.astype(jnp.float32)
        for a in range(kernel):
            for b in range(kernel):
                image_grad = (
                    image_grad
                    + conv_weight[:, a, b][None, :, None, None]
                    * d_padded[:, :, 6 - a : 6 - a + rows, 6 - b : 6 - b + cols]
                )
        return image_grad.astype(jnp.bfloat16)

    taps = []
    for a in range(kernel):
        for b in range(kernel):
            taps.append(jnp.sum(d_conv * padded[:, :, a : a + rows, b : b + cols], axis=(0, 2, 3)))
    pixel_count = slides_here * lax.axis_size("slide") * rows * lax.axis_size("strip") * cols
    scale = 1.0 / math.sqrt(float(pixel_count))
    terms = (
        jnp.stack(taps, axis=0),
        jnp.sum(d_conv, axis=(0, 2, 3)),
        jnp.sum(d_lifted * normed, axis=(0, 2, 3)),
        jnp.sum(d_lifted, axis=(0, 2, 3)),
        jnp.einsum("scrw,sfrw->cf", lifted, d_pre, preferred_element_type=jnp.float32),
        jnp.sum(d_pre.astype(jnp.float32), axis=(0, 2, 3)),
        jnp.einsum("scrw,sfrw->cf", d_branch, act, preferred_element_type=jnp.float32),
        jnp.sum(d_branch.astype(jnp.float32), axis=(0, 2, 3)),
        jnp.sum(upstream * branch, axis=(0, 2, 3)),
    )
    g, image_grad = tree_psum(
        [item * scale for item in terms], image_grad_of, (d_padded, cotangent)
    )
    g[0] = g[0].reshape(kernel, kernel, chans).transpose(2, 0, 1)
    g[6] = g[6].T
    return (image_grad, g[0], g[1], g[2], g[3], g[4], g[5], g[6], g[7], g[8])


def solution(mesh):
    in_specs = (
        P("slide", None, "strip", None),
        P("slide", None, "strip", None),
        P(),
        P(),
        P(),
        P(),
        P(),
        P(),
        P(),
        P(),
        P(),
    )
    out_specs = (P("slide", None, "strip", None), P(), P(), P(), P(), P(), P(), P(), P(), P())
    return jax.shard_map(
        on_device, mesh=mesh, in_specs=in_specs, out_specs=out_specs, check_vma=False
    )
```

```python
import math

import jax
import jax.numpy as jnp
from jax import lax
from jax.sharding import PartitionSpec as P


def with_halo(array, sides, width, whole=False):
    for axis, dim in sides:
        size, length = (lax.axis_size(axis), array.shape[dim])
        up = [(i, (i + 1) % size) for i in range(size - 1)]
        down = [(j, i) for i, j in up]
        if whole:
            before = lax.ppermute(array, axis, up)
            after = lax.ppermute(array, axis, down)
            before = lax.slice_in_dim(before, length - width, length, axis=dim)
            after = lax.slice_in_dim(after, 0, width, axis=dim)
            array = jnp.concatenate([before, array, after], axis=dim)
            continue
        last = lax.slice_in_dim(array, length - width, length, axis=dim)
        first = lax.slice_in_dim(array, 0, width, axis=dim)
        before = lax.ppermute(last, axis, up)
        after = lax.ppermute(first, axis, down)
        array = jnp.concatenate([before, array, after], axis=dim)
    return array


def xor_pairs(size, mask):
    return [(i, i ^ mask) for i in range(size)]


def low_bits(size):
    bits = []
    bit = 1
    while bit < size:
        bits.append(bit)
        bit *= 2
    return bits


def tree_psum(terms, side_fn, side_in):
    shapes = [t.shape for t in terms]
    sizes = [math.prod(s) for s in shapes]
    rooms = [-(-size // 1024) * 1024 for size in sizes]
    total = sum(rooms)
    strip_bits = low_bits(lax.axis_size("strip"))
    slide_bits = low_bits(lax.axis_size("slide"))
    scatter = [("strip", b) for b in strip_bits[:2]]
    stages = [("slide", slide_bits[i : i + 2]) for i in range(0, len(slide_bits), 2)]
    stages += [("strip", [b]) for b in strip_bits[2:]]
    pieces = 2 ** len(scatter)
    rows = -(-total // (pieces * 128))
    rows = -(-rows // 8) * 8
    flat = jnp.concatenate([jnp.pad(t.reshape(-1), (0, room - size)) for t, size, room in zip(terms, sizes, rooms)])
    flat = jnp.pad(flat, (0, pieces * rows * 128 - total)).reshape(pieces, rows, 128)
    for axis, bit in scatter:
        size = lax.axis_size(axis)
        half = flat.shape[0] // 2
        mine = (lax.axis_index(axis) // bit) % 2
        keep = lax.dynamic_slice_in_dim(flat, mine * half, half, axis=0)
        give = lax.dynamic_slice_in_dim(flat, (1 - mine) * half, half, axis=0)
        flat = keep + lax.ppermute(give, axis, xor_pairs(size, bit))
    for axis, bits in stages:
        size = lax.axis_size(axis)
        masks = []
        for m in range(1, 2 ** len(bits)):
            masks.append(sum(b for k, b in enumerate(bits) if (m >> k) & 1))
        got = [lax.ppermute(flat, axis, xor_pairs(size, mask)) for mask in masks]
        for item in got:
            flat = flat + item
    flat, side_in = lax.optimization_barrier((flat, side_in))
    hold = side_fn(*side_in)
    for step, (axis, bit) in enumerate(reversed(scatter)):
        if step == len(scatter) - 1:
            flat, hold = lax.optimization_barrier((flat, hold))
        size = lax.axis_size(axis)
        mine = (lax.axis_index(axis) // bit) % 2
        got = lax.ppermute(flat, axis, xor_pairs(size, bit))
        low = jnp.where(mine == 0, flat, got)
        high = jnp.where(mine == 0, got, flat)
        flat = jnp.concatenate([low, high], axis=0)
    flat = flat.reshape(-1)
    out = []
    offset = 0
    for shape, size, room in zip(shapes, sizes, rooms):
        out.append(flat[offset : offset + size].reshape(shape))
        offset += room
    return out, hold


def gelu_slope(value):
    return 0.5 * (1.0 + jax.scipy.special.erf(value / math.sqrt(2.0))) + value * jnp.exp(
        -0.5 * value * value
    ) / math.sqrt(2.0 * math.pi)


def on_device(
    images,
    cotangent,
    conv_weight,
    conv_bias,
    norm_gain,
    norm_bias,
    up_weight,
    up_bias,
    down_weight,
    down_bias,
    layer_scale,
):
    slides_here = images.shape[0]
    chans = images.shape[1]
    rows = images.shape[2]
    cols = images.shape[3]
    kernel = conv_weight.shape[1]
    extended = with_halo(images, (("strip", 2),), 3, whole=True)
    upstream = cotangent.astype(jnp.float32)
    padded = jnp.pad(extended, ((0, 0), (0, 0), (0, 0), (3, 3)))
    conv = lax.conv_general_dilated(
        extended.astype(jnp.float32),
        conv_weight[:, None],
        window_strides=(1, 1),
        padding=((0, 0), (3, 3)),
        dimension_numbers=("NCHW", "OIHW", "NCHW"),
        feature_group_count=chans,
        precision=lax.Precision.HIGHEST,
    ) + conv_bias[None, :, None, None]
    centre = conv - jnp.mean(conv, axis=1, keepdims=True)
    inv = lax.rsqrt(jnp.mean(centre * centre, axis=1, keepdims=True) + 1e-06)
    normed = centre * inv
    lifted = (normed * norm_gain[None, :, None, None] + norm_bias[None, :, None, None]).astype(
        jnp.bfloat16
    )
    pre = (
        jnp.einsum("scrw,cf->sfrw", lifted, up_weight, preferred_element_type=jnp.float32)
        + up_bias[None, :, None, None]
    )
    act = jax.nn.gelu(pre, approximate=False).astype(jnp.bfloat16)
    branch = (
        jnp.einsum("sfrw,fc->scrw", act, down_weight, preferred_element_type=jnp.float32)
        + down_bias[None, :, None, None]
    )
    d_branch = (layer_scale[None, :, None, None] * upstream).astype(jnp.bfloat16)
    d_act = jnp.einsum("scrw,fc->sfrw", d_branch, down_weight, preferred_element_type=jnp.float32)
    d_pre = (d_act * gelu_slope(pre)).astype(jnp.bfloat16)
    d_lifted = jnp.einsum("sfrw,cf->scrw", d_pre, up_weight, preferred_element_type=jnp.float32)
    d_normed = d_lifted * norm_gain[None, :, None, None]
    d_conv = inv * (
        d_normed
        - jnp.mean(d_normed, axis=1, keepdims=True)
        - normed * jnp.mean(d_normed * normed, axis=1, keepdims=True)
    )
    d_wide = with_halo(d_conv, (("strip", 2),), 3)
    d_padded = jnp.pad(d_wide, ((0, 0), (0, 0), (0, 0), (3, 3)))
    def image_grad_of(d_padded, cotangent):
        image_grad = cotangent.astype(jnp.float32)
        for a in range(kernel):
            for b in range(kernel):
                image_grad = (
                    image_grad
                    + conv_weight[:, a, b][None, :, None, None]
                    * d_padded[:, :, 6 - a : 6 - a + rows, 6 - b : 6 - b + cols]
                )
        return image_grad.astype(jnp.bfloat16)

    taps = []
    for a in range(kernel):
        for b in range(kernel):
            taps.append(jnp.sum(d_conv * padded[:, :, a : a + rows, b : b + cols], axis=(0, 2, 3)))
    pixel_count = slides_here * lax.axis_size("slide") * rows * lax.axis_size("strip") * cols
    scale = 1.0 / math.sqrt(float(pixel_count))
    terms = (
        jnp.stack(taps, axis=0),
        jnp.sum(d_conv, axis=(0, 2, 3)),
        jnp.sum(d_lifted * normed, axis=(0, 2, 3)),
        jnp.sum(d_lifted, axis=(0, 2, 3)),
        jnp.einsum("scrw,sfrw->cf", lifted, d_pre, preferred_element_type=jnp.float32),
        jnp.sum(d_pre.astype(jnp.float32), axis=(0, 2, 3)),
        jnp.einsum("scrw,sfrw->cf", d_branch, act, preferred_element_type=jnp.float32),
        jnp.sum(d_branch.astype(jnp.float32), axis=(0, 2, 3)),
        jnp.sum(upstream * branch, axis=(0, 2, 3)),
    )
    g, image_grad = tree_psum(
        [item * scale for item in terms], image_grad_of, (d_padded, cotangent)
    )
    g[0] = g[0].reshape(kernel, kernel, chans).transpose(2, 0, 1)
    g[6] = g[6].T
    return (image_grad, g[0], g[1], g[2], g[3], g[4], g[5], g[6], g[7], g[8])


def solution(mesh):
    in_specs = (
        P("slide", None, "strip", None),
        P("slide", None, "strip", None),
        P(),
        P(),
        P(),
        P(),
        P(),
        P(),
        P(),
        P(),
        P(),
    )
    out_specs = (P("slide", None, "strip", None), P(), P(), P(), P(), P(), P(), P(), P(), P())
    return jax.shard_map(
        on_device, mesh=mesh, in_specs=in_specs, out_specs=out_specs, check_vma=False
    )
```

```python
import math

import jax
import jax.numpy as jnp
from jax import lax
from jax.sharding import PartitionSpec as P


def with_halo(array, sides, width, whole=False):
    for axis, dim in sides:
        size, length = (lax.axis_size(axis), array.shape[dim])
        up = [(i, (i + 1) % size) for i in range(size - 1)]
        down = [(j, i) for i, j in up]
        if whole:
            before = lax.ppermute(array, axis, up)
            after = lax.ppermute(array, axis, down)
            before = lax.slice_in_dim(before, length - width, length, axis=dim)
            after = lax.slice_in_dim(after, 0, width, axis=dim)
            array = jnp.concatenate([before, array, after], axis=dim)
            continue
        last = lax.slice_in_dim(array, length - width, length, axis=dim)
        first = lax.slice_in_dim(array, 0, width, axis=dim)
        before = lax.ppermute(last, axis, up)
        after = lax.ppermute(first, axis, down)
        array = jnp.concatenate([before, array, after], axis=dim)
    return array


def xor_pairs(size, mask):
    return [(i, i ^ mask) for i in range(size)]


def low_bits(size):
    bits = []
    bit = 1
    while bit < size:
        bits.append(bit)
        bit *= 2
    return bits


def tree_psum(terms, side_fn, side_in):
    shapes = [t.shape for t in terms]
    sizes = [math.prod(s) for s in shapes]
    rooms = [-(-size // 1024) * 1024 for size in sizes]
    total = sum(rooms)
    strip_bits = low_bits(lax.axis_size("strip"))
    slide_bits = low_bits(lax.axis_size("slide"))
    scatter = [("strip", b) for b in strip_bits[:2]]
    stages = [("slide", slide_bits[i : i + 2]) for i in range(0, len(slide_bits), 2)]
    stages += [("strip", [b]) for b in strip_bits[2:]]
    pieces = 2 ** len(scatter)
    rows = -(-total // (pieces * 128))
    rows = -(-rows // 8) * 8
    flat = jnp.concatenate([jnp.pad(t.reshape(-1), (0, room - size)) for t, size, room in zip(terms, sizes, rooms)])
    flat = jnp.pad(flat, (0, pieces * rows * 128 - total)).reshape(pieces, rows, 128)
    for axis, bit in scatter:
        size = lax.axis_size(axis)
        half = flat.shape[0] // 2
        mine = (lax.axis_index(axis) // bit) % 2
        keep = lax.dynamic_slice_in_dim(flat, mine * half, half, axis=0)
        give = lax.dynamic_slice_in_dim(flat, (1 - mine) * half, half, axis=0)
        flat = keep + lax.ppermute(give, axis, xor_pairs(size, bit))
    for axis, bits in stages:
        size = lax.axis_size(axis)
        masks = []
        for m in range(1, 2 ** len(bits)):
            masks.append(sum(b for k, b in enumerate(bits) if (m >> k) & 1))
        got = [lax.ppermute(flat, axis, xor_pairs(size, mask)) for mask in masks]
        for item in got:
            flat = flat + item
    flat, side_in = lax.optimization_barrier((flat, side_in))
    hold = side_fn(*side_in)
    for step, (axis, bit) in enumerate(reversed(scatter)):
        if step == len(scatter) - 1:
            flat, hold = lax.optimization_barrier((flat, hold))
        size = lax.axis_size(axis)
        mine = (lax.axis_index(axis) // bit) % 2
        got = lax.ppermute(flat, axis, xor_pairs(size, bit))
        low = jnp.where(mine == 0, flat, got)
        high = jnp.where(mine == 0, got, flat)
        flat = jnp.concatenate([low, high], axis=0)
    flat = flat.reshape(-1)
    out = []
    offset = 0
    for shape, size, room in zip(shapes, sizes, rooms):
        out.append(flat[offset : offset + size].reshape(shape))
        offset += room
    return out, hold


def gelu_slope(value):
    return 0.5 * (1.0 + jax.scipy.special.erf(value / math.sqrt(2.0))) + value * jnp.exp(
        -0.5 * value * value
    ) / math.sqrt(2.0 * math.pi)


def on_device(
    images,
    cotangent,
    conv_weight,
    conv_bias,
    norm_gain,
    norm_bias,
    up_weight,
    up_bias,
    down_weight,
    down_bias,
    layer_scale,
):
    slides_here = images.shape[0]
    chans = images.shape[1]
    rows = images.shape[2]
    cols = images.shape[3]
    kernel = conv_weight.shape[1]
    extended = with_halo(images, (("strip", 2),), 3, whole=True)
    upstream = cotangent.astype(jnp.float32)
    padded = jnp.pad(extended, ((0, 0), (0, 0), (0, 0), (3, 3)))
    def depthwise(weight):
        return lax.conv_general_dilated(
            extended.astype(jnp.float32),
            weight[:, None],
            window_strides=(1, 1),
            padding=((0, 0), (3, 3)),
            dimension_numbers=("NCHW", "OIHW", "NCHW"),
            feature_group_count=chans,
            precision=lax.Precision.HIGHEST,
        )

    conv, weight_vjp = jax.vjp(depthwise, conv_weight)
    conv = conv + conv_bias[None, :, None, None]
    centre = conv - jnp.mean(conv, axis=1, keepdims=True)
    inv = lax.rsqrt(jnp.mean(centre * centre, axis=1, keepdims=True) + 1e-06)
    normed = centre * inv
    lifted = (normed * norm_gain[None, :, None, None] + norm_bias[None, :, None, None]).astype(
        jnp.bfloat16
    )
    pre = (
        jnp.einsum("scrw,cf->sfrw", lifted, up_weight, preferred_element_type=jnp.float32)
        + up_bias[None, :, None, None]
    )
    act = jax.nn.gelu(pre, approximate=False).astype(jnp.bfloat16)
    branch = (
        jnp.einsum("sfrw,fc->scrw", act, down_weight, preferred_element_type=jnp.float32)
        + down_bias[None, :, None, None]
    )
    d_branch = (layer_scale[None, :, None, None] * upstream).astype(jnp.bfloat16)
    d_act = jnp.einsum("scrw,fc->sfrw", d_branch, down_weight, preferred_element_type=jnp.float32)
    d_pre = (d_act * gelu_slope(pre)).astype(jnp.bfloat16)
    d_lifted = jnp.einsum("sfrw,cf->scrw", d_pre, up_weight, preferred_element_type=jnp.float32)
    d_normed = d_lifted * norm_gain[None, :, None, None]
    d_conv = inv * (
        d_normed
        - jnp.mean(d_normed, axis=1, keepdims=True)
        - normed * jnp.mean(d_normed * normed, axis=1, keepdims=True)
    )
    d_wide = with_halo(d_conv, (("strip", 2),), 3)
    d_padded = jnp.pad(d_wide, ((0, 0), (0, 0), (0, 0), (3, 3)))
    def image_grad_of(d_padded, cotangent):
        image_grad = cotangent.astype(jnp.float32)
        for a in range(kernel):
            for b in range(kernel):
                image_grad = (
                    image_grad
                    + conv_weight[:, a, b][None, :, None, None]
                    * d_padded[:, :, 6 - a : 6 - a + rows, 6 - b : 6 - b + cols]
                )
        return image_grad.astype(jnp.bfloat16)

    (kernel_grad,) = weight_vjp(d_conv)
    pixel_count = slides_here * lax.axis_size("slide") * rows * lax.axis_size("strip") * cols
    scale = 1.0 / math.sqrt(float(pixel_count))
    terms = (
        kernel_grad.transpose(1, 2, 0),
        jnp.sum(d_conv, axis=(0, 2, 3)),
        jnp.sum(d_lifted * normed, axis=(0, 2, 3)),
        jnp.sum(d_lifted, axis=(0, 2, 3)),
        jnp.einsum("scrw,sfrw->cf", lifted, d_pre, preferred_element_type=jnp.float32),
        jnp.sum(d_pre.astype(jnp.float32), axis=(0, 2, 3)),
        jnp.einsum("scrw,sfrw->cf", d_branch, act, preferred_element_type=jnp.float32),
        jnp.sum(d_branch.astype(jnp.float32), axis=(0, 2, 3)),
        jnp.sum(upstream * branch, axis=(0, 2, 3)),
    )
    g, image_grad = tree_psum(
        [item * scale for item in terms], image_grad_of, (d_padded, cotangent)
    )
    g[0] = g[0].reshape(kernel, kernel, chans).transpose(2, 0, 1)
    g[6] = g[6].T
    return (image_grad, g[0], g[1], g[2], g[3], g[4], g[5], g[6], g[7], g[8])


def solution(mesh):
    in_specs = (
        P("slide", None, "strip", None),
        P("slide", None, "strip", None),
        P(),
        P(),
        P(),
        P(),
        P(),
        P(),
        P(),
        P(),
        P(),
    )
    out_specs = (P("slide", None, "strip", None), P(), P(), P(), P(), P(), P(), P(), P(), P())
    return jax.shard_map(
        on_device, mesh=mesh, in_specs=in_specs, out_specs=out_specs, check_vma=False
    )
```

```python
import math

import jax
import jax.numpy as jnp
from jax import lax
from jax.sharding import PartitionSpec as P


def with_halo(array, sides, width, whole=False):
    for axis, dim in sides:
        size, length = (lax.axis_size(axis), array.shape[dim])
        up = [(i, (i + 1) % size) for i in range(size - 1)]
        down = [(j, i) for i, j in up]
        if whole:
            pairs = [(i, i + 1) for i in range(1, size - 1, 2)]
            pairs += [(j, i) for i, j in pairs]
            from_pair = lax.ppermute(array, axis, [(i, i ^ 1) for i in range(size)])
            from_chip = lax.ppermute(array, axis, pairs)
            even = lax.axis_index(axis) % 2 == 0
            above = jnp.where(even, from_chip, from_pair)
            below = jnp.where(even, from_pair, from_chip)
            before = lax.slice_in_dim(above, length - width, length, axis=dim)
            after = lax.slice_in_dim(below, 0, width, axis=dim)
            array = jnp.concatenate([before, array, after], axis=dim)
            continue
        last = lax.slice_in_dim(array, length - width, length, axis=dim)
        first = lax.slice_in_dim(array, 0, width, axis=dim)
        before = lax.ppermute(last, axis, up)
        after = lax.ppermute(first, axis, down)
        array = jnp.concatenate([before, array, after], axis=dim)
    return array


def xor_pairs(size, mask):
    return [(i, i ^ mask) for i in range(size)]


def low_bits(size):
    bits = []
    bit = 1
    while bit < size:
        bits.append(bit)
        bit *= 2
    return bits


def tree_psum(terms, side_fn, side_in):
    shapes = [t.shape for t in terms]
    sizes = [math.prod(s) for s in shapes]
    rooms = [-(-size // 1024) * 1024 for size in sizes]
    total = sum(rooms)
    strip_bits = low_bits(lax.axis_size("strip"))
    slide_bits = low_bits(lax.axis_size("slide"))
    scatter = [("strip", b) for b in strip_bits[:2]]
    stages = [("slide", slide_bits[i : i + 2]) for i in range(0, len(slide_bits), 2)]
    stages += [("strip", [b]) for b in strip_bits[2:]]
    pieces = 2 ** len(scatter)
    rows = -(-total // (pieces * 128))
    rows = -(-rows // 8) * 8
    flat = jnp.concatenate([jnp.pad(t.reshape(-1), (0, room - size)) for t, size, room in zip(terms, sizes, rooms)])
    flat = jnp.pad(flat, (0, pieces * rows * 128 - total)).reshape(pieces, rows, 128)
    for axis, bit in scatter:
        size = lax.axis_size(axis)
        half = flat.shape[0] // 2
        mine = (lax.axis_index(axis) // bit) % 2
        keep = lax.dynamic_slice_in_dim(flat, mine * half, half, axis=0)
        give = lax.dynamic_slice_in_dim(flat, (1 - mine) * half, half, axis=0)
        flat = keep + lax.ppermute(give, axis, xor_pairs(size, bit))
    for axis, bits in stages:
        size = lax.axis_size(axis)
        masks = []
        for m in range(1, 2 ** len(bits)):
            masks.append(sum(b for k, b in enumerate(bits) if (m >> k) & 1))
        got = [lax.ppermute(flat, axis, xor_pairs(size, mask)) for mask in masks]
        for item in got:
            flat = flat + item
    flat, side_in = lax.optimization_barrier((flat, side_in))
    hold = side_fn(*side_in)
    for step, (axis, bit) in enumerate(reversed(scatter)):
        if step == len(scatter) - 1:
            flat, hold = lax.optimization_barrier((flat, hold))
        size = lax.axis_size(axis)
        mine = (lax.axis_index(axis) // bit) % 2
        got = lax.ppermute(flat, axis, xor_pairs(size, bit))
        low = jnp.where(mine == 0, flat, got)
        high = jnp.where(mine == 0, got, flat)
        flat = jnp.concatenate([low, high], axis=0)
    flat = flat.reshape(-1)
    out = []
    offset = 0
    for shape, size, room in zip(shapes, sizes, rooms):
        out.append(flat[offset : offset + size].reshape(shape))
        offset += room
    return out, hold


def gelu_slope(value):
    return 0.5 * (1.0 + jax.scipy.special.erf(value / math.sqrt(2.0))) + value * jnp.exp(
        -0.5 * value * value
    ) / math.sqrt(2.0 * math.pi)


def on_device(
    images,
    cotangent,
    conv_weight,
    conv_bias,
    norm_gain,
    norm_bias,
    up_weight,
    up_bias,
    down_weight,
    down_bias,
    layer_scale,
):
    slides_here = images.shape[0]
    chans = images.shape[1]
    rows = images.shape[2]
    cols = images.shape[3]
    kernel = conv_weight.shape[1]
    extended = with_halo(images, (("strip", 2),), 3, whole=True)
    upstream = cotangent.astype(jnp.float32)
    padded = jnp.pad(extended, ((0, 0), (0, 0), (0, 0), (3, 3)))
    conv = lax.conv_general_dilated(
        extended.astype(jnp.float32),
        conv_weight[:, None],
        window_strides=(1, 1),
        padding=((0, 0), (3, 3)),
        dimension_numbers=("NCHW", "OIHW", "NCHW"),
        feature_group_count=chans,
        precision=lax.Precision.HIGHEST,
    ) + conv_bias[None, :, None, None]
    centre = conv - jnp.mean(conv, axis=1, keepdims=True)
    inv = lax.rsqrt(jnp.mean(centre * centre, axis=1, keepdims=True) + 1e-06)
    normed = centre * inv
    lifted = (normed * norm_gain[None, :, None, None] + norm_bias[None, :, None, None]).astype(
        jnp.bfloat16
    )
    pre = (
        jnp.einsum("scrw,cf->sfrw", lifted, up_weight, preferred_element_type=jnp.float32)
        + up_bias[None, :, None, None]
    )
    act = jax.nn.gelu(pre, approximate=False).astype(jnp.bfloat16)
    branch = (
        jnp.einsum("sfrw,fc->scrw", act, down_weight, preferred_element_type=jnp.float32)
        + down_bias[None, :, None, None]
    )
    d_branch = (layer_scale[None, :, None, None] * upstream).astype(jnp.bfloat16)
    d_act = jnp.einsum("scrw,fc->sfrw", d_branch, down_weight, preferred_element_type=jnp.float32)
    d_pre = (d_act * gelu_slope(pre)).astype(jnp.bfloat16)
    d_lifted = jnp.einsum("sfrw,cf->scrw", d_pre, up_weight, preferred_element_type=jnp.float32)
    d_normed = d_lifted * norm_gain[None, :, None, None]
    d_conv = inv * (
        d_normed
        - jnp.mean(d_normed, axis=1, keepdims=True)
        - normed * jnp.mean(d_normed * normed, axis=1, keepdims=True)
    )
    d_wide = with_halo(d_conv, (("strip", 2),), 3)
    d_padded = jnp.pad(d_wide, ((0, 0), (0, 0), (0, 0), (3, 3)))
    def image_grad_of(d_padded, cotangent):
        image_grad = cotangent.astype(jnp.float32)
        for a in range(kernel):
            for b in range(kernel):
                image_grad = (
                    image_grad
                    + conv_weight[:, a, b][None, :, None, None]
                    * d_padded[:, :, 6 - a : 6 - a + rows, 6 - b : 6 - b + cols]
                )
        return image_grad.astype(jnp.bfloat16)

    taps = []
    for a in range(kernel):
        for b in range(kernel):
            taps.append(jnp.sum(d_conv * padded[:, :, a : a + rows, b : b + cols], axis=(0, 2, 3)))
    pixel_count = slides_here * lax.axis_size("slide") * rows * lax.axis_size("strip") * cols
    scale = 1.0 / math.sqrt(float(pixel_count))
    terms = (
        jnp.stack(taps, axis=0),
        jnp.sum(d_conv, axis=(0, 2, 3)),
        jnp.sum(d_lifted * normed, axis=(0, 2, 3)),
        jnp.sum(d_lifted, axis=(0, 2, 3)),
        jnp.einsum("scrw,sfrw->cf", lifted, d_pre, preferred_element_type=jnp.float32),
        jnp.sum(d_pre.astype(jnp.float32), axis=(0, 2, 3)),
        jnp.einsum("scrw,sfrw->cf", d_branch, act, preferred_element_type=jnp.float32),
        jnp.sum(d_branch.astype(jnp.float32), axis=(0, 2, 3)),
        jnp.sum(upstream * branch, axis=(0, 2, 3)),
    )
    g, image_grad = tree_psum(
        [item * scale for item in terms], image_grad_of, (d_padded, cotangent)
    )
    g[0] = g[0].reshape(kernel, kernel, chans).transpose(2, 0, 1)
    g[6] = g[6].T
    return (image_grad, g[0], g[1], g[2], g[3], g[4], g[5], g[6], g[7], g[8])


def solution(mesh):
    in_specs = (
        P("slide", None, "strip", None),
        P("slide", None, "strip", None),
        P(),
        P(),
        P(),
        P(),
        P(),
        P(),
        P(),
        P(),
        P(),
    )
    out_specs = (P("slide", None, "strip", None), P(), P(), P(), P(), P(), P(), P(), P(), P())
    return jax.shard_map(
        on_device, mesh=mesh, in_specs=in_specs, out_specs=out_specs, check_vma=False
    )
```

```python
import math

import jax
import jax.numpy as jnp
from jax import lax
from jax.sharding import PartitionSpec as P


def with_halo(array, sides, width, whole=False):
    for axis, dim in sides:
        size, length = (lax.axis_size(axis), array.shape[dim])
        if whole:
            pairs = [(i, i + 1) for i in range(1, size - 1, 2)]
            pairs += [(j, i) for i, j in pairs]
            from_pair = lax.ppermute(array, axis, [(i, i ^ 1) for i in range(size)])
            from_chip = lax.ppermute(array, axis, pairs)
            even = lax.axis_index(axis) % 2 == 0
            above = jnp.where(even, from_chip, from_pair)
            below = jnp.where(even, from_pair, from_chip)
            before = lax.slice_in_dim(above, length - width, length, axis=dim)
            after = lax.slice_in_dim(below, 0, width, axis=dim)
            array = jnp.concatenate([before, array, after], axis=dim)
            continue
        last = lax.slice_in_dim(array, length - width, length, axis=dim)
        first = lax.slice_in_dim(array, 0, width, axis=dim)
        pairs = [(i, i + 1) for i in range(1, size - 1, 2)]
        pairs += [(j, i) for i, j in pairs]
        even = lax.axis_index(axis) % 2 == 0
        from_pair = lax.ppermute(jnp.where(even, last, first), axis, [(i, i ^ 1) for i in range(size)])
        from_chip = lax.ppermute(jnp.where(even, first, last), axis, pairs)
        before = jnp.where(even, from_chip, from_pair)
        after = jnp.where(even, from_pair, from_chip)
        array = jnp.concatenate([before, array, after], axis=dim)
    return array


def xor_pairs(size, mask):
    return [(i, i ^ mask) for i in range(size)]


def low_bits(size):
    bits = []
    bit = 1
    while bit < size:
        bits.append(bit)
        bit *= 2
    return bits


def tree_psum(terms, side_fn, side_in):
    shapes = [t.shape for t in terms]
    sizes = [math.prod(s) for s in shapes]
    rooms = [-(-size // 1024) * 1024 for size in sizes]
    total = sum(rooms)
    strip_bits = low_bits(lax.axis_size("strip"))
    slide_bits = low_bits(lax.axis_size("slide"))
    scatter = [("strip", b) for b in strip_bits[:2]]
    stages = [("slide", slide_bits[i : i + 2]) for i in range(0, len(slide_bits), 2)]
    stages += [("strip", [b]) for b in strip_bits[2:]]
    pieces = 2 ** len(scatter)
    rows = -(-total // (pieces * 128))
    rows = -(-rows // 8) * 8
    flat = jnp.concatenate([jnp.pad(t.reshape(-1), (0, room - size)) for t, size, room in zip(terms, sizes, rooms)])
    flat = jnp.pad(flat, (0, pieces * rows * 128 - total)).reshape(pieces, rows, 128)
    for axis, bit in scatter:
        size = lax.axis_size(axis)
        half = flat.shape[0] // 2
        mine = (lax.axis_index(axis) // bit) % 2
        keep = lax.dynamic_slice_in_dim(flat, mine * half, half, axis=0)
        give = lax.dynamic_slice_in_dim(flat, (1 - mine) * half, half, axis=0)
        flat = keep + lax.ppermute(give, axis, xor_pairs(size, bit))
    for axis, bits in stages:
        size = lax.axis_size(axis)
        masks = []
        for m in range(1, 2 ** len(bits)):
            masks.append(sum(b for k, b in enumerate(bits) if (m >> k) & 1))
        got = [lax.ppermute(flat, axis, xor_pairs(size, mask)) for mask in masks]
        for item in got:
            flat = flat + item
    flat, side_in = lax.optimization_barrier((flat, side_in))
    hold = side_fn(*side_in)
    for step, (axis, bit) in enumerate(reversed(scatter)):
        if step == len(scatter) - 1:
            flat, hold = lax.optimization_barrier((flat, hold))
        size = lax.axis_size(axis)
        mine = (lax.axis_index(axis) // bit) % 2
        got = lax.ppermute(flat, axis, xor_pairs(size, bit))
        low = jnp.where(mine == 0, flat, got)
        high = jnp.where(mine == 0, got, flat)
        flat = jnp.concatenate([low, high], axis=0)
    flat = flat.reshape(-1)
    out = []
    offset = 0
    for shape, size, room in zip(shapes, sizes, rooms):
        out.append(flat[offset : offset + size].reshape(shape))
        offset += room
    return out, hold


def gelu_slope(value):
    return 0.5 * (1.0 + jax.scipy.special.erf(value / math.sqrt(2.0))) + value * jnp.exp(
        -0.5 * value * value
    ) / math.sqrt(2.0 * math.pi)


def on_device(
    images,
    cotangent,
    conv_weight,
    conv_bias,
    norm_gain,
    norm_bias,
    up_weight,
    up_bias,
    down_weight,
    down_bias,
    layer_scale,
):
    slides_here = images.shape[0]
    chans = images.shape[1]
    rows = images.shape[2]
    cols = images.shape[3]
    kernel = conv_weight.shape[1]
    extended = with_halo(images, (("strip", 2),), 3, whole=True)
    upstream = cotangent.astype(jnp.float32)
    padded = jnp.pad(extended, ((0, 0), (0, 0), (0, 0), (3, 3)))
    conv = lax.conv_general_dilated(
        extended.astype(jnp.float32),
        conv_weight[:, None],
        window_strides=(1, 1),
        padding=((0, 0), (3, 3)),
        dimension_numbers=("NCHW", "OIHW", "NCHW"),
        feature_group_count=chans,
        precision=lax.Precision.HIGHEST,
    ) + conv_bias[None, :, None, None]
    centre = conv - jnp.mean(conv, axis=1, keepdims=True)
    inv = lax.rsqrt(jnp.mean(centre * centre, axis=1, keepdims=True) + 1e-06)
    normed = centre * inv
    lifted = (normed * norm_gain[None, :, None, None] + norm_bias[None, :, None, None]).astype(
        jnp.bfloat16
    )
    pre = (
        jnp.einsum("scrw,cf->sfrw", lifted, up_weight, preferred_element_type=jnp.float32)
        + up_bias[None, :, None, None]
    )
    act = jax.nn.gelu(pre, approximate=False).astype(jnp.bfloat16)
    branch = (
        jnp.einsum("sfrw,fc->scrw", act, down_weight, preferred_element_type=jnp.float32)
        + down_bias[None, :, None, None]
    )
    d_branch = (layer_scale[None, :, None, None] * upstream).astype(jnp.bfloat16)
    d_act = jnp.einsum("scrw,fc->sfrw", d_branch, down_weight, preferred_element_type=jnp.float32)
    d_pre = (d_act * gelu_slope(pre)).astype(jnp.bfloat16)
    d_lifted = jnp.einsum("sfrw,cf->scrw", d_pre, up_weight, preferred_element_type=jnp.float32)
    d_normed = d_lifted * norm_gain[None, :, None, None]
    d_conv = inv * (
        d_normed
        - jnp.mean(d_normed, axis=1, keepdims=True)
        - normed * jnp.mean(d_normed * normed, axis=1, keepdims=True)
    )
    d_wide = with_halo(d_conv, (("strip", 2),), 3)
    d_padded = jnp.pad(d_wide, ((0, 0), (0, 0), (0, 0), (3, 3)))
    def image_grad_of(d_padded, cotangent):
        image_grad = cotangent.astype(jnp.float32)
        for a in range(kernel):
            for b in range(kernel):
                image_grad = (
                    image_grad
                    + conv_weight[:, a, b][None, :, None, None]
                    * d_padded[:, :, 6 - a : 6 - a + rows, 6 - b : 6 - b + cols]
                )
        return image_grad.astype(jnp.bfloat16)

    taps = []
    for a in range(kernel):
        for b in range(kernel):
            taps.append(jnp.sum(d_conv * padded[:, :, a : a + rows, b : b + cols], axis=(0, 2, 3)))
    pixel_count = slides_here * lax.axis_size("slide") * rows * lax.axis_size("strip") * cols
    scale = 1.0 / math.sqrt(float(pixel_count))
    terms = (
        jnp.stack(taps, axis=0),
        jnp.sum(d_conv, axis=(0, 2, 3)),
        jnp.sum(d_lifted * normed, axis=(0, 2, 3)),
        jnp.sum(d_lifted, axis=(0, 2, 3)),
        jnp.einsum("scrw,sfrw->cf", lifted, d_pre, preferred_element_type=jnp.float32),
        jnp.sum(d_pre.astype(jnp.float32), axis=(0, 2, 3)),
        jnp.einsum("scrw,sfrw->cf", d_branch, act, preferred_element_type=jnp.float32),
        jnp.sum(d_branch.astype(jnp.float32), axis=(0, 2, 3)),
        jnp.sum(upstream * branch, axis=(0, 2, 3)),
    )
    g, image_grad = tree_psum(
        [item * scale for item in terms], image_grad_of, (d_padded, cotangent)
    )
    g[0] = g[0].reshape(kernel, kernel, chans).transpose(2, 0, 1)
    g[6] = g[6].T
    return (image_grad, g[0], g[1], g[2], g[3], g[4], g[5], g[6], g[7], g[8])


def solution(mesh):
    in_specs = (
        P("slide", None, "strip", None),
        P("slide", None, "strip", None),
        P(),
        P(),
        P(),
        P(),
        P(),
        P(),
        P(),
        P(),
        P(),
    )
    out_specs = (P("slide", None, "strip", None), P(), P(), P(), P(), P(), P(), P(), P(), P())
    return jax.shard_map(
        on_device, mesh=mesh, in_specs=in_specs, out_specs=out_specs, check_vma=False
    )
```

```python
import math

import jax
import jax.numpy as jnp
from jax import lax
from jax.sharding import PartitionSpec as P


def with_halo(array, sides, width, whole=False, pair_after=None):
    for axis, dim in sides:
        size, length = (lax.axis_size(axis), array.shape[dim])
        if whole:
            pairs = [(i, i + 1) for i in range(1, size - 1, 2)]
            pairs += [(j, i) for i, j in pairs]
            from_chip = lax.ppermute(array, axis, pairs)
            paired = array
            if pair_after is not None:
                paired, _ = lax.optimization_barrier((array, pair_after))
            from_pair = lax.ppermute(paired, axis, [(i, i ^ 1) for i in range(size)])
            even = lax.axis_index(axis) % 2 == 0
            above = jnp.where(even, from_chip, from_pair)
            below = jnp.where(even, from_pair, from_chip)
            before = lax.slice_in_dim(above, length - width, length, axis=dim)
            after = lax.slice_in_dim(below, 0, width, axis=dim)
            array = jnp.concatenate([before, array, after], axis=dim)
            continue
        last = lax.slice_in_dim(array, length - width, length, axis=dim)
        first = lax.slice_in_dim(array, 0, width, axis=dim)
        pairs = [(i, i + 1) for i in range(1, size - 1, 2)]
        pairs += [(j, i) for i, j in pairs]
        even = lax.axis_index(axis) % 2 == 0
        from_pair = lax.ppermute(jnp.where(even, last, first), axis, [(i, i ^ 1) for i in range(size)])
        from_chip = lax.ppermute(jnp.where(even, first, last), axis, pairs)
        before = jnp.where(even, from_chip, from_pair)
        after = jnp.where(even, from_pair, from_chip)
        array = jnp.concatenate([before, array, after], axis=dim)
    return array


def xor_pairs(size, mask):
    return [(i, i ^ mask) for i in range(size)]


def low_bits(size):
    bits = []
    bit = 1
    while bit < size:
        bits.append(bit)
        bit *= 2
    return bits


def tree_psum(terms, side_fn, side_in):
    shapes = [t.shape for t in terms]
    sizes = [math.prod(s) for s in shapes]
    rooms = [-(-size // 1024) * 1024 for size in sizes]
    total = sum(rooms)
    strip_bits = low_bits(lax.axis_size("strip"))
    slide_bits = low_bits(lax.axis_size("slide"))
    scatter = [("strip", b) for b in strip_bits[:2]]
    stages = [("slide", slide_bits[i : i + 2]) for i in range(0, len(slide_bits), 2)]
    stages += [("strip", [b]) for b in strip_bits[2:]]
    pieces = 2 ** len(scatter)
    rows = -(-total // (pieces * 128))
    rows = -(-rows // 8) * 8
    flat = jnp.concatenate([jnp.pad(t.reshape(-1), (0, room - size)) for t, size, room in zip(terms, sizes, rooms)])
    flat = jnp.pad(flat, (0, pieces * rows * 128 - total)).reshape(pieces, rows, 128)
    for axis, bit in scatter:
        size = lax.axis_size(axis)
        half = flat.shape[0] // 2
        mine = (lax.axis_index(axis) // bit) % 2
        keep = lax.dynamic_slice_in_dim(flat, mine * half, half, axis=0)
        give = lax.dynamic_slice_in_dim(flat, (1 - mine) * half, half, axis=0)
        flat = keep + lax.ppermute(give, axis, xor_pairs(size, bit))
    for axis, bits in stages:
        size = lax.axis_size(axis)
        masks = []
        for m in range(1, 2 ** len(bits)):
            masks.append(sum(b for k, b in enumerate(bits) if (m >> k) & 1))
        got = [lax.ppermute(flat, axis, xor_pairs(size, mask)) for mask in masks]
        for item in got:
            flat = flat + item
    flat, side_in = lax.optimization_barrier((flat, side_in))
    hold = side_fn(*side_in)
    for step, (axis, bit) in enumerate(reversed(scatter)):
        if step == len(scatter) - 1:
            flat, hold = lax.optimization_barrier((flat, hold))
        size = lax.axis_size(axis)
        mine = (lax.axis_index(axis) // bit) % 2
        got = lax.ppermute(flat, axis, xor_pairs(size, bit))
        low = jnp.where(mine == 0, flat, got)
        high = jnp.where(mine == 0, got, flat)
        flat = jnp.concatenate([low, high], axis=0)
    flat = flat.reshape(-1)
    out = []
    offset = 0
    for shape, size, room in zip(shapes, sizes, rooms):
        out.append(flat[offset : offset + size].reshape(shape))
        offset += room
    return out, hold


def gelu_slope(value):
    return 0.5 * (1.0 + jax.scipy.special.erf(value / math.sqrt(2.0))) + value * jnp.exp(
        -0.5 * value * value
    ) / math.sqrt(2.0 * math.pi)


def on_device(
    images,
    cotangent,
    conv_weight,
    conv_bias,
    norm_gain,
    norm_bias,
    up_weight,
    up_bias,
    down_weight,
    down_bias,
    layer_scale,
):
    slides_here = images.shape[0]
    chans = images.shape[1]
    rows = images.shape[2]
    cols = images.shape[3]
    kernel = conv_weight.shape[1]
    upstream = cotangent.astype(jnp.float32)
    d_branch = (layer_scale[None, :, None, None] * upstream).astype(jnp.bfloat16)
    d_branch_sum = jnp.sum(d_branch.astype(jnp.float32), axis=(0, 2, 3))
    extended = with_halo(images, (("strip", 2),), 3, whole=True, pair_after=d_branch_sum)
    upstream = cotangent.astype(jnp.float32)
    padded = jnp.pad(extended, ((0, 0), (0, 0), (0, 0), (3, 3)))
    conv = lax.conv_general_dilated(
        extended.astype(jnp.float32),
        conv_weight[:, None],
        window_strides=(1, 1),
        padding=((0, 0), (3, 3)),
        dimension_numbers=("NCHW", "OIHW", "NCHW"),
        feature_group_count=chans,
        precision=lax.Precision.HIGHEST,
    ) + conv_bias[None, :, None, None]
    centre = conv - jnp.mean(conv, axis=1, keepdims=True)
    inv = lax.rsqrt(jnp.mean(centre * centre, axis=1, keepdims=True) + 1e-06)
    normed = centre * inv
    lifted = (normed * norm_gain[None, :, None, None] + norm_bias[None, :, None, None]).astype(
        jnp.bfloat16
    )
    pre = (
        jnp.einsum("scrw,cf->sfrw", lifted, up_weight, preferred_element_type=jnp.float32)
        + up_bias[None, :, None, None]
    )
    act = jax.nn.gelu(pre, approximate=False).astype(jnp.bfloat16)
    branch = (
        jnp.einsum("sfrw,fc->scrw", act, down_weight, preferred_element_type=jnp.float32)
        + down_bias[None, :, None, None]
    )
    d_act = jnp.einsum("scrw,fc->sfrw", d_branch, down_weight, preferred_element_type=jnp.float32)
    d_pre = (d_act * gelu_slope(pre)).astype(jnp.bfloat16)
    d_lifted = jnp.einsum("sfrw,cf->scrw", d_pre, up_weight, preferred_element_type=jnp.float32)
    d_normed = d_lifted * norm_gain[None, :, None, None]
    d_conv = inv * (
        d_normed
        - jnp.mean(d_normed, axis=1, keepdims=True)
        - normed * jnp.mean(d_normed * normed, axis=1, keepdims=True)
    )
    d_wide = with_halo(d_conv, (("strip", 2),), 3)
    d_padded = jnp.pad(d_wide, ((0, 0), (0, 0), (0, 0), (3, 3)))
    def image_grad_of(d_padded, cotangent):
        image_grad = cotangent.astype(jnp.float32)
        for a in range(kernel):
            for b in range(kernel):
                image_grad = (
                    image_grad
                    + conv_weight[:, a, b][None, :, None, None]
                    * d_padded[:, :, 6 - a : 6 - a + rows, 6 - b : 6 - b + cols]
                )
        return image_grad.astype(jnp.bfloat16)

    taps = []
    for a in range(kernel):
        for b in range(kernel):
            taps.append(jnp.sum(d_conv * padded[:, :, a : a + rows, b : b + cols], axis=(0, 2, 3)))
    pixel_count = slides_here * lax.axis_size("slide") * rows * lax.axis_size("strip") * cols
    scale = 1.0 / math.sqrt(float(pixel_count))
    terms = (
        jnp.stack(taps, axis=0),
        jnp.sum(d_conv, axis=(0, 2, 3)),
        jnp.sum(d_lifted * normed, axis=(0, 2, 3)),
        jnp.sum(d_lifted, axis=(0, 2, 3)),
        jnp.einsum("scrw,sfrw->cf", lifted, d_pre, preferred_element_type=jnp.float32),
        jnp.sum(d_pre.astype(jnp.float32), axis=(0, 2, 3)),
        jnp.einsum("scrw,sfrw->cf", d_branch, act, preferred_element_type=jnp.float32),
        d_branch_sum,
        jnp.sum(upstream * branch, axis=(0, 2, 3)),
    )
    g, image_grad = tree_psum(
        [item * scale for item in terms], image_grad_of, (d_padded, cotangent)
    )
    g[0] = g[0].reshape(kernel, kernel, chans).transpose(2, 0, 1)
    g[6] = g[6].T
    return (image_grad, g[0], g[1], g[2], g[3], g[4], g[5], g[6], g[7], g[8])


def solution(mesh):
    in_specs = (
        P("slide", None, "strip", None),
        P("slide", None, "strip", None),
        P(),
        P(),
        P(),
        P(),
        P(),
        P(),
        P(),
        P(),
        P(),
    )
    out_specs = (P("slide", None, "strip", None), P(), P(), P(), P(), P(), P(), P(), P(), P())
    return jax.shard_map(
        on_device, mesh=mesh, in_specs=in_specs, out_specs=out_specs, check_vma=False
    )
```

```python
import math

import jax
import jax.numpy as jnp
from jax import lax
from jax.sharding import PartitionSpec as P


def with_halo(array, sides, width, whole=False):
    for axis, dim in sides:
        size, length = (lax.axis_size(axis), array.shape[dim])
        if whole:
            pairs = [(i, i + 1) for i in range(1, size - 1, 2)]
            pairs += [(j, i) for i, j in pairs]
            from_pair = lax.ppermute(array, axis, [(i, i ^ 1) for i in range(size)])
            from_chip = lax.ppermute(array, axis, pairs)
            even = lax.axis_index(axis) % 2 == 0
            above = jnp.where(even, from_chip, from_pair)
            below = jnp.where(even, from_pair, from_chip)
            before = lax.slice_in_dim(above, length - width, length, axis=dim)
            after = lax.slice_in_dim(below, 0, width, axis=dim)
            array = jnp.concatenate([before, array, after], axis=dim)
            continue
        last = lax.slice_in_dim(array, length - width, length, axis=dim)
        first = lax.slice_in_dim(array, 0, width, axis=dim)
        pairs = [(i, i + 1) for i in range(1, size - 1, 2)]
        pairs += [(j, i) for i, j in pairs]
        even = lax.axis_index(axis) % 2 == 0
        from_pair = lax.ppermute(jnp.where(even, last, first), axis, [(i, i ^ 1) for i in range(size)])
        from_chip = lax.ppermute(jnp.where(even, first, last), axis, pairs)
        before = jnp.where(even, from_chip, from_pair)
        after = jnp.where(even, from_pair, from_chip)
        array = jnp.concatenate([before, array, after], axis=dim)
    return array


def xor_pairs(size, mask):
    return [(i, i ^ mask) for i in range(size)]


def low_bits(size):
    bits = []
    bit = 1
    while bit < size:
        bits.append(bit)
        bit *= 2
    return bits


def tree_psum(terms, side_fn, side_in):
    shapes = [t.shape for t in terms]
    sizes = [math.prod(s) for s in shapes]
    rooms = [-(-size // 1024) * 1024 for size in sizes]
    total = sum(rooms)
    strip_bits = low_bits(lax.axis_size("strip"))
    slide_bits = low_bits(lax.axis_size("slide"))
    scatter = [("strip", b) for b in strip_bits[:2]]
    stages = [("slide", slide_bits[i : i + 2]) for i in range(0, len(slide_bits), 2)]
    stages += [("strip", [b]) for b in strip_bits[2:]]
    pieces = 2 ** len(scatter)
    rows = -(-total // (pieces * 128))
    rows = -(-rows // 8) * 8
    flat = jnp.concatenate([jnp.pad(t.reshape(-1), (0, room - size)) for t, size, room in zip(terms, sizes, rooms)])
    flat = jnp.pad(flat, (0, pieces * rows * 128 - total)).reshape(pieces, rows, 128)
    for axis, bit in scatter:
        size = lax.axis_size(axis)
        half = flat.shape[0] // 2
        mine = (lax.axis_index(axis) // bit) % 2
        keep = lax.dynamic_slice_in_dim(flat, mine * half, half, axis=0)
        give = lax.dynamic_slice_in_dim(flat, (1 - mine) * half, half, axis=0)
        flat = keep + lax.ppermute(give, axis, xor_pairs(size, bit))
    for axis, bits in stages:
        size = lax.axis_size(axis)
        masks = []
        for m in range(1, 2 ** len(bits)):
            masks.append(sum(b for k, b in enumerate(bits) if (m >> k) & 1))
        got = [lax.ppermute(flat, axis, xor_pairs(size, mask)) for mask in masks]
        for item in got:
            flat = flat + item
    flat, side_in = lax.optimization_barrier((flat, side_in))
    hold = side_fn(*side_in)
    for step, (axis, bit) in enumerate(reversed(scatter)):
        if step == len(scatter) - 1:
            flat, hold = lax.optimization_barrier((flat, hold))
        size = lax.axis_size(axis)
        mine = (lax.axis_index(axis) // bit) % 2
        got = lax.ppermute(flat, axis, xor_pairs(size, bit))
        low = jnp.where(mine == 0, flat, got)
        high = jnp.where(mine == 0, got, flat)
        flat = jnp.concatenate([low, high], axis=0)
    flat = flat.reshape(-1)
    out = []
    offset = 0
    for shape, size, room in zip(shapes, sizes, rooms):
        out.append(flat[offset : offset + size].reshape(shape))
        offset += room
    return out, hold


def gelu_slope(value):
    return 0.5 * (1.0 + jax.scipy.special.erf(value / math.sqrt(2.0))) + value * jnp.exp(
        -0.5 * value * value
    ) / math.sqrt(2.0 * math.pi)


def on_device(
    images,
    cotangent,
    conv_weight,
    conv_bias,
    norm_gain,
    norm_bias,
    up_weight,
    up_bias,
    down_weight,
    down_bias,
    layer_scale,
):
    slides_here = images.shape[0]
    chans = images.shape[1]
    rows = images.shape[2]
    cols = images.shape[3]
    kernel = conv_weight.shape[1]
    extended = with_halo(images, (("strip", 2),), 3, whole=True)
    upstream = cotangent.astype(jnp.float32)
    padded = jnp.pad(extended, ((0, 0), (0, 0), (0, 0), (3, 3)))
    conv = lax.conv_general_dilated(
        extended.astype(jnp.float32),
        conv_weight[:, None],
        window_strides=(1, 1),
        padding=((0, 0), (3, 3)),
        dimension_numbers=("NCHW", "OIHW", "NCHW"),
        feature_group_count=chans,
        precision=lax.Precision.HIGHEST,
    ) + conv_bias[None, :, None, None]
    centre = conv - jnp.mean(conv, axis=1, keepdims=True)
    inv = lax.rsqrt(jnp.mean(centre * centre, axis=1, keepdims=True) + 1e-06)
    normed = centre * inv
    lifted = (normed * norm_gain[None, :, None, None] + norm_bias[None, :, None, None]).astype(
        jnp.bfloat16
    )
    pre = (
        jnp.einsum("scrw,cf->sfrw", lifted, up_weight, preferred_element_type=jnp.float32)
        + up_bias[None, :, None, None]
    )
    act = jax.nn.gelu(pre, approximate=False).astype(jnp.bfloat16)
    branch = (
        jnp.einsum("sfrw,fc->scrw", act, down_weight, preferred_element_type=jnp.float32)
        + down_bias[None, :, None, None]
    )
    d_branch = (layer_scale[None, :, None, None] * upstream).astype(jnp.bfloat16)
    d_act = jnp.einsum("scrw,fc->sfrw", d_branch, down_weight, preferred_element_type=jnp.float32)
    d_pre = (d_act * gelu_slope(pre)).astype(jnp.bfloat16)
    d_lifted = jnp.einsum("sfrw,cf->scrw", d_pre, up_weight, preferred_element_type=jnp.float32)
    d_normed = d_lifted * norm_gain[None, :, None, None]
    d_conv = inv * (
        d_normed
        - jnp.mean(d_normed, axis=1, keepdims=True)
        - normed * jnp.mean(d_normed * normed, axis=1, keepdims=True)
    )
    d_wide = with_halo(d_conv, (("strip", 2),), 3)
    def image_grad_of(d_wide, cotangent):
        spread = lax.conv_general_dilated(
            d_wide,
            conv_weight[:, ::-1, ::-1][:, None],
            window_strides=(1, 1),
            padding=((0, 0), (3, 3)),
            dimension_numbers=("NCHW", "OIHW", "NCHW"),
            feature_group_count=chans,
            precision=lax.Precision.HIGHEST,
        )
        image_grad = cotangent.astype(jnp.float32) + spread
        return image_grad.astype(jnp.bfloat16)

    taps = []
    for a in range(kernel):
        for b in range(kernel):
            taps.append(jnp.sum(d_conv * padded[:, :, a : a + rows, b : b + cols], axis=(0, 2, 3)))
    pixel_count = slides_here * lax.axis_size("slide") * rows * lax.axis_size("strip") * cols
    scale = 1.0 / math.sqrt(float(pixel_count))
    terms = (
        jnp.stack(taps, axis=0),
        jnp.sum(d_conv, axis=(0, 2, 3)),
        jnp.sum(d_lifted * normed, axis=(0, 2, 3)),
        jnp.sum(d_lifted, axis=(0, 2, 3)),
        jnp.einsum("scrw,sfrw->cf", lifted, d_pre, preferred_element_type=jnp.float32),
        jnp.sum(d_pre.astype(jnp.float32), axis=(0, 2, 3)),
        jnp.einsum("scrw,sfrw->cf", d_branch, act, preferred_element_type=jnp.float32),
        jnp.sum(d_branch.astype(jnp.float32), axis=(0, 2, 3)),
        jnp.sum(upstream * branch, axis=(0, 2, 3)),
    )
    g, image_grad = tree_psum(
        [item * scale for item in terms], image_grad_of, (d_wide, cotangent)
    )
    g[0] = g[0].reshape(kernel, kernel, chans).transpose(2, 0, 1)
    g[6] = g[6].T
    return (image_grad, g[0], g[1], g[2], g[3], g[4], g[5], g[6], g[7], g[8])


def solution(mesh):
    in_specs = (
        P("slide", None, "strip", None),
        P("slide", None, "strip", None),
        P(),
        P(),
        P(),
        P(),
        P(),
        P(),
        P(),
        P(),
        P(),
    )
    out_specs = (P("slide", None, "strip", None), P(), P(), P(), P(), P(), P(), P(), P(), P())
    return jax.shard_map(
        on_device, mesh=mesh, in_specs=in_specs, out_specs=out_specs, check_vma=False
    )
```

```python
import math

import jax
import jax.numpy as jnp
from jax import lax
from jax.sharding import PartitionSpec as P


def with_halo(array, sides, width, whole=False, pair_after=None):
    for axis, dim in sides:
        size, length = (lax.axis_size(axis), array.shape[dim])
        if whole:
            pairs = [(i, i + 1) for i in range(1, size - 1, 2)]
            pairs += [(j, i) for i, j in pairs]
            from_chip = lax.ppermute(array, axis, pairs)
            paired = array
            if pair_after is not None:
                paired, _ = lax.optimization_barrier((array, pair_after))
            from_pair = lax.ppermute(paired, axis, [(i, i ^ 1) for i in range(size)])
            even = lax.axis_index(axis) % 2 == 0
            above = jnp.where(even, from_chip, from_pair)
            below = jnp.where(even, from_pair, from_chip)
            before = lax.slice_in_dim(above, length - width, length, axis=dim)
            after = lax.slice_in_dim(below, 0, width, axis=dim)
            array = jnp.concatenate([before, array, after], axis=dim)
            continue
        last = lax.slice_in_dim(array, length - width, length, axis=dim)
        first = lax.slice_in_dim(array, 0, width, axis=dim)
        pairs = [(i, i + 1) for i in range(1, size - 1, 2)]
        pairs += [(j, i) for i, j in pairs]
        even = lax.axis_index(axis) % 2 == 0
        from_pair = lax.ppermute(jnp.where(even, last, first), axis, [(i, i ^ 1) for i in range(size)])
        from_chip = lax.ppermute(jnp.where(even, first, last), axis, pairs)
        before = jnp.where(even, from_chip, from_pair)
        after = jnp.where(even, from_pair, from_chip)
        array = jnp.concatenate([before, array, after], axis=dim)
    return array


def xor_pairs(size, mask):
    return [(i, i ^ mask) for i in range(size)]


def low_bits(size):
    bits = []
    bit = 1
    while bit < size:
        bits.append(bit)
        bit *= 2
    return bits


def tree_psum(terms, side_fn, side_in):
    shapes = [t.shape for t in terms]
    sizes = [math.prod(s) for s in shapes]
    rooms = [-(-size // 1024) * 1024 for size in sizes]
    total = sum(rooms)
    strip_bits = low_bits(lax.axis_size("strip"))
    slide_bits = low_bits(lax.axis_size("slide"))
    scatter = [("strip", b) for b in strip_bits[:2]]
    stages = [("slide", slide_bits[i : i + 2]) for i in range(0, len(slide_bits), 2)]
    stages += [("strip", [b]) for b in strip_bits[2:]]
    pieces = 2 ** len(scatter)
    rows = -(-total // (pieces * 128))
    rows = -(-rows // 8) * 8
    flat = jnp.concatenate([jnp.pad(t.reshape(-1), (0, room - size)) for t, size, room in zip(terms, sizes, rooms)])
    flat = jnp.pad(flat, (0, pieces * rows * 128 - total)).reshape(pieces, rows, 128)
    for axis, bit in scatter:
        size = lax.axis_size(axis)
        half = flat.shape[0] // 2
        mine = (lax.axis_index(axis) // bit) % 2
        keep = lax.dynamic_slice_in_dim(flat, mine * half, half, axis=0)
        give = lax.dynamic_slice_in_dim(flat, (1 - mine) * half, half, axis=0)
        flat = keep + lax.ppermute(give, axis, xor_pairs(size, bit))
    for axis, bits in stages:
        size = lax.axis_size(axis)
        masks = []
        for m in range(1, 2 ** len(bits)):
            masks.append(sum(b for k, b in enumerate(bits) if (m >> k) & 1))
        got = [lax.ppermute(flat, axis, xor_pairs(size, mask)) for mask in masks]
        for item in got:
            flat = flat + item
    flat, side_in = lax.optimization_barrier((flat, side_in))
    hold = side_fn(*side_in)
    for step, (axis, bit) in enumerate(reversed(scatter)):
        if step == len(scatter) - 1:
            flat, hold = lax.optimization_barrier((flat, hold))
        size = lax.axis_size(axis)
        mine = (lax.axis_index(axis) // bit) % 2
        got = lax.ppermute(flat, axis, xor_pairs(size, bit))
        low = jnp.where(mine == 0, flat, got)
        high = jnp.where(mine == 0, got, flat)
        flat = jnp.concatenate([low, high], axis=0)
    flat = flat.reshape(-1)
    out = []
    offset = 0
    for shape, size, room in zip(shapes, sizes, rooms):
        out.append(flat[offset : offset + size].reshape(shape))
        offset += room
    return out, hold


def gelu_slope(value):
    return 0.5 * (1.0 + jax.scipy.special.erf(value / math.sqrt(2.0))) + value * jnp.exp(
        -0.5 * value * value
    ) / math.sqrt(2.0 * math.pi)


def on_device(
    images,
    cotangent,
    conv_weight,
    conv_bias,
    norm_gain,
    norm_bias,
    up_weight,
    up_bias,
    down_weight,
    down_bias,
    layer_scale,
):
    slides_here = images.shape[0]
    chans = images.shape[1]
    rows = images.shape[2]
    cols = images.shape[3]
    kernel = conv_weight.shape[1]
    upstream = cotangent.astype(jnp.float32)
    d_branch = (layer_scale[None, :, None, None] * upstream).astype(jnp.bfloat16)
    d_branch_sum = jnp.sum(d_branch.astype(jnp.float32), axis=(0, 2, 3))
    extended = with_halo(images, (("strip", 2),), 3, whole=True, pair_after=d_branch_sum)
    upstream = cotangent.astype(jnp.float32)
    padded = jnp.pad(extended, ((0, 0), (0, 0), (0, 0), (3, 3)))
    conv = lax.conv_general_dilated(
        extended.astype(jnp.float32),
        conv_weight[:, None],
        window_strides=(1, 1),
        padding=((0, 0), (3, 3)),
        dimension_numbers=("NCHW", "OIHW", "NCHW"),
        feature_group_count=chans,
        precision=lax.Precision.HIGHEST,
    ) + conv_bias[None, :, None, None]
    centre = conv - jnp.mean(conv, axis=1, keepdims=True)
    inv = lax.rsqrt(jnp.mean(centre * centre, axis=1, keepdims=True) + 1e-06)
    normed = centre * inv
    lifted = (normed * norm_gain[None, :, None, None] + norm_bias[None, :, None, None]).astype(
        jnp.bfloat16
    )
    pre = (
        jnp.einsum("scrw,cf->sfrw", lifted, up_weight, preferred_element_type=jnp.float32)
        + up_bias[None, :, None, None]
    )
    act = jax.nn.gelu(pre, approximate=False).astype(jnp.bfloat16)
    branch = (
        jnp.einsum("sfrw,fc->scrw", act, down_weight, preferred_element_type=jnp.float32)
        + down_bias[None, :, None, None]
    )
    d_act = jnp.einsum("scrw,fc->sfrw", d_branch, down_weight, preferred_element_type=jnp.float32)
    d_pre = (d_act * gelu_slope(pre)).astype(jnp.bfloat16)
    d_lifted = jnp.einsum("sfrw,cf->scrw", d_pre, up_weight, preferred_element_type=jnp.float32)
    d_normed = d_lifted * norm_gain[None, :, None, None]
    d_conv = inv * (
        d_normed
        - jnp.mean(d_normed, axis=1, keepdims=True)
        - normed * jnp.mean(d_normed * normed, axis=1, keepdims=True)
    )
    d_wide = with_halo(d_conv, (("strip", 2),), 3)
    def image_grad_of(d_wide, cotangent):
        spread = lax.conv_general_dilated(
            d_wide,
            conv_weight[:, ::-1, ::-1][:, None],
            window_strides=(1, 1),
            padding=((0, 0), (3, 3)),
            dimension_numbers=("NCHW", "OIHW", "NCHW"),
            feature_group_count=chans,
            precision=lax.Precision.HIGHEST,
        )
        image_grad = cotangent.astype(jnp.float32) + spread
        return image_grad.astype(jnp.bfloat16)

    taps = []
    for a in range(kernel):
        for b in range(kernel):
            taps.append(jnp.sum(d_conv * padded[:, :, a : a + rows, b : b + cols], axis=(0, 2, 3)))
    pixel_count = slides_here * lax.axis_size("slide") * rows * lax.axis_size("strip") * cols
    scale = 1.0 / math.sqrt(float(pixel_count))
    terms = (
        jnp.stack(taps, axis=0),
        jnp.sum(d_conv, axis=(0, 2, 3)),
        jnp.sum(d_lifted * normed, axis=(0, 2, 3)),
        jnp.sum(d_lifted, axis=(0, 2, 3)),
        jnp.einsum("scrw,sfrw->cf", lifted, d_pre, preferred_element_type=jnp.float32),
        jnp.sum(d_pre.astype(jnp.float32), axis=(0, 2, 3)),
        jnp.einsum("scrw,sfrw->cf", d_branch, act, preferred_element_type=jnp.float32),
        d_branch_sum,
        jnp.sum(upstream * branch, axis=(0, 2, 3)),
    )
    g, image_grad = tree_psum(
        [item * scale for item in terms], image_grad_of, (d_wide, cotangent)
    )
    g[0] = g[0].reshape(kernel, kernel, chans).transpose(2, 0, 1)
    g[6] = g[6].T
    return (image_grad, g[0], g[1], g[2], g[3], g[4], g[5], g[6], g[7], g[8])


def solution(mesh):
    in_specs = (
        P("slide", None, "strip", None),
        P("slide", None, "strip", None),
        P(),
        P(),
        P(),
        P(),
        P(),
        P(),
        P(),
        P(),
        P(),
    )
    out_specs = (P("slide", None, "strip", None), P(), P(), P(), P(), P(), P(), P(), P(), P())
    return jax.shard_map(
        on_device, mesh=mesh, in_specs=in_specs, out_specs=out_specs, check_vma=False
    )
```

```python
import math

import jax
import jax.numpy as jnp
from jax import lax
from jax.sharding import PartitionSpec as P


def with_halo(array, sides, width, whole=False, pair_after=None):
    for axis, dim in sides:
        size, length = (lax.axis_size(axis), array.shape[dim])
        if whole:
            pairs = [(i, i + 1) for i in range(1, size - 1, 2)]
            pairs += [(j, i) for i, j in pairs]
            from_chip = lax.ppermute(array, axis, pairs)
            paired = array
            if pair_after is not None:
                paired, _ = lax.optimization_barrier((array, pair_after))
            from_pair = lax.ppermute(paired, axis, [(i, i ^ 1) for i in range(size)])
            even = lax.axis_index(axis) % 2 == 0
            above = jnp.where(even, from_chip, from_pair)
            below = jnp.where(even, from_pair, from_chip)
            before = lax.slice_in_dim(above, length - width, length, axis=dim)
            after = lax.slice_in_dim(below, 0, width, axis=dim)
            array = jnp.concatenate([before, array, after], axis=dim)
            continue
        last = lax.slice_in_dim(array, length - width, length, axis=dim)
        first = lax.slice_in_dim(array, 0, width, axis=dim)
        pairs = [(i, i + 1) for i in range(1, size - 1, 2)]
        pairs += [(j, i) for i, j in pairs]
        even = lax.axis_index(axis) % 2 == 0
        from_pair = lax.ppermute(jnp.where(even, last, first), axis, [(i, i ^ 1) for i in range(size)])
        from_chip = lax.ppermute(jnp.where(even, first, last), axis, pairs)
        before = jnp.where(even, from_chip, from_pair)
        after = jnp.where(even, from_pair, from_chip)
        array = jnp.concatenate([before, array, after], axis=dim)
    return array


def xor_pairs(size, mask):
    return [(i, i ^ mask) for i in range(size)]


def low_bits(size):
    bits = []
    bit = 1
    while bit < size:
        bits.append(bit)
        bit *= 2
    return bits


def tree_psum(terms, side_fn, side_in):
    shapes = [t.shape for t in terms]
    sizes = [math.prod(s) for s in shapes]
    total = sum(sizes)
    strip_bits = low_bits(lax.axis_size("strip"))
    slide_bits = low_bits(lax.axis_size("slide"))
    scatter = [("strip", b) for b in strip_bits[:2]]
    stages = [("slide", slide_bits[i : i + 2]) for i in range(0, len(slide_bits), 2)]
    stages += [("strip", [b]) for b in strip_bits[2:]]
    pieces = 2 ** len(scatter)
    rows = -(-total // (pieces * 128))
    rows = -(-rows // 8) * 8
    order = sorted(range(len(terms)), key=lambda i: -sizes[i])
    flat = jnp.concatenate([terms[i].reshape(-1) for i in order])
    flat = jnp.pad(flat, (0, pieces * rows * 128 - total)).reshape(pieces, rows, 128)
    for axis, bit in scatter:
        size = lax.axis_size(axis)
        half = flat.shape[0] // 2
        mine = (lax.axis_index(axis) // bit) % 2
        keep = lax.dynamic_slice_in_dim(flat, mine * half, half, axis=0)
        give = lax.dynamic_slice_in_dim(flat, (1 - mine) * half, half, axis=0)
        flat = keep + lax.ppermute(give, axis, xor_pairs(size, bit))
    for axis, bits in stages:
        size = lax.axis_size(axis)
        masks = []
        for m in range(1, 2 ** len(bits)):
            masks.append(sum(b for k, b in enumerate(bits) if (m >> k) & 1))
        got = [lax.ppermute(flat, axis, xor_pairs(size, mask)) for mask in masks]
        for item in got:
            flat = flat + item
    flat, side_in = lax.optimization_barrier((flat, side_in))
    hold = side_fn(*side_in)
    for step, (axis, bit) in enumerate(reversed(scatter)):
        if step == len(scatter) - 1:
            flat, hold = lax.optimization_barrier((flat, hold))
        size = lax.axis_size(axis)
        mine = (lax.axis_index(axis) // bit) % 2
        got = lax.ppermute(flat, axis, xor_pairs(size, bit))
        low = jnp.where(mine == 0, flat, got)
        high = jnp.where(mine == 0, got, flat)
        flat = jnp.concatenate([low, high], axis=0)
    flat = flat.reshape(-1)
    out = [None] * len(terms)
    offset = 0
    for i in order:
        out[i] = flat[offset : offset + sizes[i]].reshape(shapes[i])
        offset += sizes[i]
    return out, hold


def gelu_slope(value):
    return 0.5 * (1.0 + jax.scipy.special.erf(value / math.sqrt(2.0))) + value * jnp.exp(
        -0.5 * value * value
    ) / math.sqrt(2.0 * math.pi)


def on_device(
    images,
    cotangent,
    conv_weight,
    conv_bias,
    norm_gain,
    norm_bias,
    up_weight,
    up_bias,
    down_weight,
    down_bias,
    layer_scale,
):
    slides_here = images.shape[0]
    chans = images.shape[1]
    rows = images.shape[2]
    cols = images.shape[3]
    kernel = conv_weight.shape[1]
    upstream = cotangent.astype(jnp.float32)
    d_branch = (layer_scale[None, :, None, None] * upstream).astype(jnp.bfloat16)
    d_branch_sum = jnp.sum(d_branch.astype(jnp.float32), axis=(0, 2, 3))
    extended = with_halo(images, (("strip", 2),), 3, whole=True, pair_after=d_branch_sum)
    upstream = cotangent.astype(jnp.float32)
    padded = jnp.pad(extended, ((0, 0), (0, 0), (0, 0), (3, 3)))
    conv = lax.conv_general_dilated(
        extended.astype(jnp.float32),
        conv_weight[:, None],
        window_strides=(1, 1),
        padding=((0, 0), (3, 3)),
        dimension_numbers=("NCHW", "OIHW", "NCHW"),
        feature_group_count=chans,
        precision=lax.Precision.HIGHEST,
    ) + conv_bias[None, :, None, None]
    centre = conv - jnp.mean(conv, axis=1, keepdims=True)
    inv = lax.rsqrt(jnp.mean(centre * centre, axis=1, keepdims=True) + 1e-06)
    normed = centre * inv
    lifted = (normed * norm_gain[None, :, None, None] + norm_bias[None, :, None, None]).astype(
        jnp.bfloat16
    )
    pre = (
        jnp.einsum("scrw,cf->sfrw", lifted, up_weight, preferred_element_type=jnp.float32)
        + up_bias[None, :, None, None]
    )
    act = jax.nn.gelu(pre, approximate=False).astype(jnp.bfloat16)
    branch = (
        jnp.einsum("sfrw,fc->scrw", act, down_weight, preferred_element_type=jnp.float32)
        + down_bias[None, :, None, None]
    )
    d_act = jnp.einsum("scrw,fc->sfrw", d_branch, down_weight, preferred_element_type=jnp.float32)
    d_pre = (d_act * gelu_slope(pre)).astype(jnp.bfloat16)
    d_lifted = jnp.einsum("sfrw,cf->scrw", d_pre, up_weight, preferred_element_type=jnp.float32)
    d_normed = d_lifted * norm_gain[None, :, None, None]
    d_conv = inv * (
        d_normed
        - jnp.mean(d_normed, axis=1, keepdims=True)
        - normed * jnp.mean(d_normed * normed, axis=1, keepdims=True)
    )
    d_wide = with_halo(d_conv, (("strip", 2),), 3)
    def image_grad_of(d_wide, cotangent):
        spread = lax.conv_general_dilated(
            d_wide,
            conv_weight[:, ::-1, ::-1][:, None],
            window_strides=(1, 1),
            padding=((0, 0), (3, 3)),
            dimension_numbers=("NCHW", "OIHW", "NCHW"),
            feature_group_count=chans,
            precision=lax.Precision.HIGHEST,
        )
        image_grad = cotangent.astype(jnp.float32) + spread
        return image_grad.astype(jnp.bfloat16)

    taps = []
    for a in range(kernel):
        for b in range(kernel):
            taps.append(jnp.sum(d_conv * padded[:, :, a : a + rows, b : b + cols], axis=(0, 2, 3)))
    pixel_count = slides_here * lax.axis_size("slide") * rows * lax.axis_size("strip") * cols
    scale = 1.0 / math.sqrt(float(pixel_count))
    terms = (
        jnp.stack(taps, axis=0),
        jnp.sum(d_conv, axis=(0, 2, 3)),
        jnp.sum(d_lifted * normed, axis=(0, 2, 3)),
        jnp.sum(d_lifted, axis=(0, 2, 3)),
        jnp.einsum("scrw,sfrw->cf", lifted, d_pre, preferred_element_type=jnp.float32),
        jnp.sum(d_pre.astype(jnp.float32), axis=(0, 2, 3)),
        jnp.einsum("scrw,sfrw->cf", d_branch, act, preferred_element_type=jnp.float32),
        d_branch_sum,
        jnp.sum(upstream * branch, axis=(0, 2, 3)),
    )
    g, image_grad = tree_psum(
        [item * scale for item in terms], image_grad_of, (d_wide, cotangent)
    )
    g[0] = g[0].reshape(kernel, kernel, chans).transpose(2, 0, 1)
    g[6] = g[6].T
    return (image_grad, g[0], g[1], g[2], g[3], g[4], g[5], g[6], g[7], g[8])


def solution(mesh):
    in_specs = (
        P("slide", None, "strip", None),
        P("slide", None, "strip", None),
        P(),
        P(),
        P(),
        P(),
        P(),
        P(),
        P(),
        P(),
        P(),
    )
    out_specs = (P("slide", None, "strip", None), P(), P(), P(), P(), P(), P(), P(), P(), P())
    return jax.shard_map(
        on_device, mesh=mesh, in_specs=in_specs, out_specs=out_specs, check_vma=False
    )
```

```python
import math

import jax
import jax.numpy as jnp
from jax import lax
from jax.sharding import PartitionSpec as P


def with_halo(array, sides, width, whole=False, pair_after=None):
    for axis, dim in sides:
        size, length = (lax.axis_size(axis), array.shape[dim])
        if whole:
            pairs = [(i, i + 1) for i in range(1, size - 1, 2)]
            pairs += [(j, i) for i, j in pairs]
            from_chip = lax.ppermute(array, axis, pairs)
            paired = array
            if pair_after is not None:
                paired, _ = lax.optimization_barrier((array, pair_after))
            from_pair = lax.ppermute(paired, axis, [(i, i ^ 1) for i in range(size)])
            even = lax.axis_index(axis) % 2 == 0
            above = jnp.where(even, from_chip, from_pair)
            below = jnp.where(even, from_pair, from_chip)
            before = lax.slice_in_dim(above, length - width, length, axis=dim)
            after = lax.slice_in_dim(below, 0, width, axis=dim)
            array = jnp.concatenate([before, array, after], axis=dim)
            continue
        last = lax.slice_in_dim(array, length - width, length, axis=dim)
        first = lax.slice_in_dim(array, 0, width, axis=dim)
        pairs = [(i, i + 1) for i in range(1, size - 1, 2)]
        pairs += [(j, i) for i, j in pairs]
        even = lax.axis_index(axis) % 2 == 0
        from_pair = lax.ppermute(jnp.where(even, last, first), axis, [(i, i ^ 1) for i in range(size)])
        from_chip = lax.ppermute(jnp.where(even, first, last), axis, pairs)
        before = jnp.where(even, from_chip, from_pair)
        after = jnp.where(even, from_pair, from_chip)
        array = jnp.concatenate([before, array, after], axis=dim)
    return array


def xor_pairs(size, mask):
    return [(i, i ^ mask) for i in range(size)]


def low_bits(size):
    bits = []
    bit = 1
    while bit < size:
        bits.append(bit)
        bit *= 2
    return bits


def tree_psum(terms, side_fn, side_in):
    shapes = [t.shape for t in terms]
    sizes = [math.prod(s) for s in shapes]
    rooms = [-(-size // 1024) * 1024 for size in sizes]
    total = sum(rooms)
    strip_bits = low_bits(lax.axis_size("strip"))
    slide_bits = low_bits(lax.axis_size("slide"))
    scatter = [("strip", b) for b in strip_bits[:2]]
    stages = [("slide", slide_bits[i : i + 2]) for i in range(0, len(slide_bits), 2)]
    stages += [("strip", [b]) for b in strip_bits[2:]]
    pieces = 2 ** len(scatter)
    rows = -(-total // (pieces * 128))
    rows = -(-rows // 8) * 8
    flat = jnp.concatenate([jnp.pad(t.reshape(-1), (0, room - size)) for t, size, room in zip(terms, sizes, rooms)])
    flat = jnp.pad(flat, (0, pieces * rows * 128 - total)).reshape(pieces, rows, 128)
    for axis, bit in scatter:
        size = lax.axis_size(axis)
        half = flat.shape[0] // 2
        mine = (lax.axis_index(axis) // bit) % 2
        keep = lax.dynamic_slice_in_dim(flat, mine * half, half, axis=0)
        give = lax.dynamic_slice_in_dim(flat, (1 - mine) * half, half, axis=0)
        flat = keep + lax.ppermute(give, axis, xor_pairs(size, bit))
    for axis, bits in stages:
        size = lax.axis_size(axis)
        masks = []
        for m in range(1, 2 ** len(bits)):
            masks.append(sum(b for k, b in enumerate(bits) if (m >> k) & 1))
        got = [lax.ppermute(flat, axis, xor_pairs(size, mask)) for mask in masks]
        for item in got:
            flat = flat + item
    flat, side_in = lax.optimization_barrier((flat, side_in))
    hold = side_fn(*side_in)
    for step, (axis, bit) in enumerate(reversed(scatter)):
        if step == len(scatter) - 1:
            flat, hold = lax.optimization_barrier((flat, hold))
        size = lax.axis_size(axis)
        mine = (lax.axis_index(axis) // bit) % 2
        got = lax.ppermute(flat, axis, xor_pairs(size, bit))
        low = jnp.where(mine == 0, flat, got)
        high = jnp.where(mine == 0, got, flat)
        flat = jnp.concatenate([low, high], axis=0)
    flat = flat.reshape(-1)
    out = []
    offset = 0
    for shape, size, room in zip(shapes, sizes, rooms):
        out.append(flat[offset : offset + size].reshape(shape))
        offset += room
    return out, hold


def gelu_slope(value):
    return 0.5 * (1.0 + jax.scipy.special.erf(value / math.sqrt(2.0))) + value * jnp.exp(
        -0.5 * value * value
    ) / math.sqrt(2.0 * math.pi)


def on_device(
    images,
    cotangent,
    conv_weight,
    conv_bias,
    norm_gain,
    norm_bias,
    up_weight,
    up_bias,
    down_weight,
    down_bias,
    layer_scale,
):
    slides_here = images.shape[0]
    chans = images.shape[1]
    rows = images.shape[2]
    cols = images.shape[3]
    kernel = conv_weight.shape[1]
    upstream = cotangent.astype(jnp.float32)
    d_branch = (layer_scale[None, :, None, None] * upstream).astype(jnp.bfloat16)
    d_branch_sum = jnp.sum(d_branch.astype(jnp.float32), axis=(0, 2, 3))
    extended = with_halo(images, (("strip", 2),), 3, whole=True, pair_after=d_branch_sum)
    d_act = jnp.einsum("scrw,fc->sfrw", d_branch, down_weight, preferred_element_type=jnp.float32)
    extended, d_act = lax.optimization_barrier((extended, d_act))
    upstream = cotangent.astype(jnp.float32)
    padded = jnp.pad(extended, ((0, 0), (0, 0), (0, 0), (3, 3)))
    conv = lax.conv_general_dilated(
        extended.astype(jnp.float32),
        conv_weight[:, None],
        window_strides=(1, 1),
        padding=((0, 0), (3, 3)),
        dimension_numbers=("NCHW", "OIHW", "NCHW"),
        feature_group_count=chans,
        precision=lax.Precision.HIGHEST,
    ) + conv_bias[None, :, None, None]
    centre = conv - jnp.mean(conv, axis=1, keepdims=True)
    inv = lax.rsqrt(jnp.mean(centre * centre, axis=1, keepdims=True) + 1e-06)
    normed = centre * inv
    lifted = (normed * norm_gain[None, :, None, None] + norm_bias[None, :, None, None]).astype(
        jnp.bfloat16
    )
    pre = (
        jnp.einsum("scrw,cf->sfrw", lifted, up_weight, preferred_element_type=jnp.float32)
        + up_bias[None, :, None, None]
    )
    act = jax.nn.gelu(pre, approximate=False).astype(jnp.bfloat16)
    branch = (
        jnp.einsum("sfrw,fc->scrw", act, down_weight, preferred_element_type=jnp.float32)
        + down_bias[None, :, None, None]
    )
    d_pre = (d_act * gelu_slope(pre)).astype(jnp.bfloat16)
    d_lifted = jnp.einsum("sfrw,cf->scrw", d_pre, up_weight, preferred_element_type=jnp.float32)
    d_normed = d_lifted * norm_gain[None, :, None, None]
    d_conv = inv * (
        d_normed
        - jnp.mean(d_normed, axis=1, keepdims=True)
        - normed * jnp.mean(d_normed * normed, axis=1, keepdims=True)
    )
    d_wide = with_halo(d_conv, (("strip", 2),), 3)
    def image_grad_of(d_wide, cotangent):
        spread = lax.conv_general_dilated(
            d_wide,
            conv_weight[:, ::-1, ::-1][:, None],
            window_strides=(1, 1),
            padding=((0, 0), (3, 3)),
            dimension_numbers=("NCHW", "OIHW", "NCHW"),
            feature_group_count=chans,
            precision=lax.Precision.HIGHEST,
        )
        image_grad = cotangent.astype(jnp.float32) + spread
        return image_grad.astype(jnp.bfloat16)

    taps = []
    for a in range(kernel):
        for b in range(kernel):
            taps.append(jnp.sum(d_conv * padded[:, :, a : a + rows, b : b + cols], axis=(0, 2, 3)))
    pixel_count = slides_here * lax.axis_size("slide") * rows * lax.axis_size("strip") * cols
    scale = 1.0 / math.sqrt(float(pixel_count))
    terms = (
        jnp.stack(taps, axis=0),
        jnp.sum(d_conv, axis=(0, 2, 3)),
        jnp.sum(d_lifted * normed, axis=(0, 2, 3)),
        jnp.sum(d_lifted, axis=(0, 2, 3)),
        jnp.einsum("scrw,sfrw->cf", lifted, d_pre, preferred_element_type=jnp.float32),
        jnp.sum(d_pre.astype(jnp.float32), axis=(0, 2, 3)),
        jnp.einsum("scrw,sfrw->cf", d_branch, act, preferred_element_type=jnp.float32),
        d_branch_sum,
        jnp.sum(upstream * branch, axis=(0, 2, 3)),
    )
    g, image_grad = tree_psum(
        [item * scale for item in terms], image_grad_of, (d_wide, cotangent)
    )
    g[0] = g[0].reshape(kernel, kernel, chans).transpose(2, 0, 1)
    g[6] = g[6].T
    return (image_grad, g[0], g[1], g[2], g[3], g[4], g[5], g[6], g[7], g[8])


def solution(mesh):
    in_specs = (
        P("slide", None, "strip", None),
        P("slide", None, "strip", None),
        P(),
        P(),
        P(),
        P(),
        P(),
        P(),
        P(),
        P(),
        P(),
    )
    out_specs = (P("slide", None, "strip", None), P(), P(), P(), P(), P(), P(), P(), P(), P())
    return jax.shard_map(
        on_device, mesh=mesh, in_specs=in_specs, out_specs=out_specs, check_vma=False
    )
```
